32 devices in a mesh: slab: 8 (over z, y), yz: 4 (over x, core).
Axes of the slice: x: 2, y: 2, z: 4, core: 2. Of those that a mesh axis runs over, the one named last changes fastest.
Arguments:
- field_e: float32 [3, 32, 32, 128], P(None, 'slab', 'yz'), may hold values from -6 to 6
- field_h: float32 [3, 32, 32, 128], P(None, 'slab', 'yz'), may hold values from -6 to 6
- permittivity: float32 [3, 32, 32, 128], P(None, 'slab', 'yz'), may hold values from 1 to 12
- conductivity: float32 [32, 32, 128], P('slab', 'yz'), may hold values from 0.02 to 1
- forward_e: float32 [8, 4, 2, 3, 64], P('slab', 'yz'), may hold values from -6 to 6
- slot_cell: int32 [8, 4, 8, 8], P('slab', 'yz'), may hold values from 0 to 4096, as said below
- recv_param: int32 [8, 4, 8, 8], P('slab', 'yz'), may hold values from 0 to 128, as said below
Outputs:
- new_e: float32 [3, 32, 32, 128], P(None, 'slab', 'yz')
- new_h: float32 [3, 32, 32, 128], P(None, 'slab', 'yz')
- gradient: float32 [8, 4, 128], P('slab', 'yz')
The draws below stay inside these ranges and needn't reach their ends.
Inputs may be any that keep to these rules, and one draw needn't show every extreme that they name: Slot c from device (s, y) to owner d of the same yz index is filled when slot_cell[s, y, d, c] < 4096, which holds exactly when recv_param[d, y, s, c] < 128; filled slots of a pair come first. In every draw one owner receives 8 filled slots from every source and some pair has no filled slot. `recv_param`: see slot_cell.
All inputs are finite; a program needn't handle non-finite values.
Results may differ from the reference program's by a relative error of at most 0.0001.
Values sent between devices are 32-bit elements; how exact they have to be, the bound alone decides.
No kernel may reach another device: no remote copies, remote signals or barrier semaphores. Data moves between devices by JAX's collectives and lax.ppermute only.
A program may use at most 64 MiB of HBM per device.

```python
import math
import jax
import jax.numpy as jnp
from jax import lax

CX = 4
CY = 8
CZ = 128
STEPS = 2
CAP = 8
PAR_DEV = 128
NX = 32
NY = 32
NZ = 128
SLOTS = 64
N_SLAB = 8
N_YZ = 4


def plan_counts(key):
    base = jax.random.fold_in(key, 7)
    key_heavy = jax.random.fold_in(base, 1)
    key_high = jax.random.fold_in(base, 2)
    key_light = jax.random.fold_in(base, 3)
    key_full = jax.random.fold_in(base, 4)
    heavy_owner = jax.random.randint(key_heavy, (N_SLAB,), 0, 2)
    heavy_count = jax.random.randint(key_high, (N_SLAB, N_YZ, N_SLAB), CAP // 2, CAP + 1)
    light_count = jax.random.randint(key_light, (N_SLAB, N_YZ, N_SLAB), 0, CAP // 2 + 1)
    counts = jnp.where(heavy_owner[None, None, :] == 1, heavy_count, light_count)
    full_owner = jax.random.randint(key_full, (), 0, N_SLAB)
    owners = jnp.arange(N_SLAB)[None, None, :]
    counts = jnp.where(owners == full_owner, CAP, counts)
    counts = jnp.where(owners == (full_owner + 1) % N_SLAB, 0, counts)
    return counts


def draw_slot_cell(key, part):
    counts = plan_counts(key)
    filled = jnp.arange(CAP)[None, None, None, :] < counts[..., None]
    cell_ids = jax.random.randint(jax.random.fold_in(key, 11), (N_SLAB, N_YZ, N_SLAB, CAP), 0, CX * CY * CZ)
    return jnp.where(filled, cell_ids, CX * CY * CZ).astype(jnp.int32)


def draw_recv_param(key, part):
    counts = plan_counts(key)
    filled = jnp.arange(CAP)[None, None, None, :] < counts[..., None]
    filled = jnp.transpose(filled, (2, 1, 0, 3))
    params = jax.random.randint(jax.random.fold_in(key, 13), (N_SLAB, N_YZ, N_SLAB, CAP), 0, PAR_DEV)
    return jnp.where(filled, params, PAR_DEV).astype(jnp.int32)


def level_of(own_key, shape, split, smallest, top_value):
    loudness = 1.0
    for position, shards_of in split:
        heights = jax.random.uniform(jax.random.fold_in(jax.random.fold_in(own_key, 6), position), (shards_of,), jnp.float32, smallest / len(split), top_value / len(split))
        loudness = loudness * jnp.repeat(jnp.exp(heights), shape[position] // shards_of).reshape((-1,) + (1,) * (len(shape) - 1 - position))
    return loudness


def gaussian(key, dims, scale, limit, split=(), kind=jnp.bfloat16):
    gain = level_of(key, dims, split, -0.22, 0.18) if split else 1.0
    entries = jax.random.normal(key, dims, jnp.float32) * scale * gain
    return jnp.minimum(jnp.maximum(entries, -limit), limit).astype(kind)


def setup_inputs(seed: int = 0) -> dict:
    seeds = jax.random.split(jax.random.key(seed), 8)
    field_e = gaussian(seeds[0], (3, NX, NY, NZ), 1.0, 6.0, ((1, 8), (2, 4)), jnp.float32)
    field_h = gaussian(seeds[1], (3, NX, NY, NZ), 1.0, 6.0, ((1, 8), (2, 4)), jnp.float32)
    permittivity = jnp.clip(jnp.exp(math.log(12.0) - 2.4849066 * jax.random.uniform(seeds[2], (3, NX, NY, NZ), jnp.float32) ** level_of(seeds[2], (3, NX, NY, NZ), ((1, 8), (2, 4)), -0.2, 0.2)), 1.0, 12.0)
    conductivity = jnp.clip(jnp.exp(math.log(1.0) - 3.912023 * jax.random.uniform(seeds[3], (NX, NY, NZ), jnp.float32) ** level_of(seeds[3], (NX, NY, NZ), ((0, 8), (1, 4)), -0.2, 0.2)), 0.02, 1.0)
    forward_e = gaussian(seeds[4], (N_SLAB, N_YZ, STEPS, 3, SLOTS), 1.0, 6.0, ((0, 8), (1, 4)), jnp.float32)
    slot_cell = draw_slot_cell(jax.random.fold_in(seeds[7], 71), 0)
    recv_param = draw_recv_param(jax.random.fold_in(seeds[7], 71), 0)
    return dict(field_e=field_e, field_h=field_h, permittivity=permittivity, conductivity=conductivity, forward_e=forward_e, slot_cell=slot_cell, recv_param=recv_param)


CH_GAIN = 0.5
CE_GAIN = 0.5


def diff_ahead(values, edges, along):
    extent = values.shape[along]
    return jnp.concatenate([lax.slice_in_dim(values, 1, extent, axis=along), edges], along) - values


def diff_behind(values, edges, along):
    extent = values.shape[along]
    return values - jnp.concatenate([edges, lax.slice_in_dim(values, 0, extent - 1, axis=along)], along)


def curl_ahead(field, x_edges, y_edges):
    z_zeros = jnp.zeros_like(field[0][:, :, 0:1])
    curl_x = diff_ahead(field[2], y_edges[1], 1) - diff_ahead(field[1], z_zeros, 2)
    curl_y = diff_ahead(field[0], z_zeros, 2) - diff_ahead(field[2], x_edges[1], 0)
    curl_z = diff_ahead(field[1], x_edges[0], 0) - diff_ahead(field[0], y_edges[0], 1)
    return jnp.stack([curl_x, curl_y, curl_z])


def curl_behind(field, x_edges, y_edges):
    z_zeros = jnp.zeros_like(field[0][:, :, 0:1])
    curl_x = diff_behind(field[2], y_edges[1], 1) - diff_behind(field[1], z_zeros, 2)
    curl_y = diff_behind(field[0], z_zeros, 2) - diff_behind(field[2], x_edges[1], 0)
    curl_z = diff_behind(field[1], x_edges[0], 0) - diff_behind(field[0], y_edges[0], 1)
    return jnp.stack([curl_x, curl_y, curl_z])


def reference(field_e, field_h, permittivity, conductivity, forward_e, slot_cell, recv_param):
    ratio = 0.5 * conductivity[None] / permittivity
    keep_rate = (1.0 - ratio) / (1.0 + ratio)
    curl_gain = CE_GAIN / (permittivity * (1.0 + ratio))
    x_zeros = jnp.zeros((2, 1, NY, NZ), field_e.dtype)
    y_zeros = jnp.zeros((2, NX, 1, NZ), field_e.dtype)
    cell_index = jnp.broadcast_to(slot_cell.reshape(1, N_SLAB, N_YZ, SLOTS), (3, N_SLAB, N_YZ, SLOTS)).astype(jnp.int32)
    owner_rows = (jnp.arange(N_SLAB, dtype=jnp.int32)[:, None, None, None] * N_YZ + jnp.arange(N_YZ, dtype=jnp.int32)[None, :, None, None]) * (PAR_DEV + 1)
    segment_ids = (owner_rows + recv_param.astype(jnp.int32)).reshape(-1)
    total = jnp.zeros((N_SLAB * N_YZ * (PAR_DEV + 1),), field_e.dtype)
    for step_index in range(STEPS):
        field_h = field_h - CH_GAIN * curl_ahead(field_e, x_zeros, y_zeros)
        field_e = keep_rate * field_e + curl_gain * curl_behind(field_h, x_zeros, y_zeros)
        local = field_e.reshape(3, N_SLAB, CX, N_YZ, CY, NZ).transpose(0, 1, 3, 2, 4, 5).reshape(3, N_SLAB, N_YZ, CX * CY * NZ)
        padded = jnp.concatenate([local, jnp.zeros((3, N_SLAB, N_YZ, 1), field_e.dtype)], 3)
        picked = jnp.take_along_axis(padded, cell_index, axis=3)
        forward_now = jnp.transpose(forward_e[:, :, step_index], (2, 0, 1, 3))
        products = jnp.sum(picked * forward_now, axis=0)
        routed = products.reshape(N_SLAB, N_YZ, N_SLAB, CAP).transpose(2, 1, 0, 3)
        total = total + jax.ops.segment_sum(routed.reshape(-1), segment_ids, num_segments=N_SLAB * N_YZ * (PAR_DEV + 1))
    gradient = total.reshape(N_SLAB, N_YZ, PAR_DEV + 1)[:, :, :PAR_DEV]
    return field_e, field_h, gradient
```

```python
import jax
import jax.numpy as jnp
from jax import lax
from jax.sharding import PartitionSpec as P

STEPS = 2
PAR_DEV = 128
HALO = 2

CH_GAIN = 0.5
CE_GAIN = 0.5


def recv_from(array, axis, offset):
    count = lax.axis_size(axis)
    pairs = [(i + offset, i) for i in range(count) if 0 <= i + offset < count]
    return lax.ppermute(array, axis, pairs)


def diff_ahead(values, along):
    extent = values.shape[along]
    edge = jnp.zeros_like(lax.slice_in_dim(values, 0, 1, axis=along))
    return jnp.concatenate([lax.slice_in_dim(values, 1, extent, axis=along), edge], along) - values


def diff_behind(values, along):
    extent = values.shape[along]
    edge = jnp.zeros_like(lax.slice_in_dim(values, 0, 1, axis=along))
    return values - jnp.concatenate([edge, lax.slice_in_dim(values, 0, extent - 1, axis=along)], along)


def curl_ahead(field):
    curl_x = diff_ahead(field[2], 1) - diff_ahead(field[1], 2)
    curl_y = diff_ahead(field[0], 2) - diff_ahead(field[2], 0)
    curl_z = diff_ahead(field[1], 0) - diff_ahead(field[0], 1)
    return jnp.stack([curl_x, curl_y, curl_z])


def curl_behind(field):
    curl_x = diff_behind(field[2], 1) - diff_behind(field[1], 2)
    curl_y = diff_behind(field[0], 2) - diff_behind(field[2], 0)
    curl_z = diff_behind(field[1], 0) - diff_behind(field[0], 1)
    return jnp.stack([curl_x, curl_y, curl_z])


def with_halo(stack, depth_x, depth_y):
    low = recv_from(stack[:, depth_x - HALO : depth_x], "slab", -1)
    high = recv_from(stack[:, 0:HALO], "slab", 1)
    stack = jnp.concatenate([low, stack, high], 1)
    low = recv_from(stack[:, :, depth_y - HALO : depth_y], "yz", -1)
    high = recv_from(stack[:, :, 0:HALO], "yz", 1)
    return jnp.concatenate([low, stack, high], 2)


def shards(field_e, field_h, permittivity, conductivity, forward_e, slot_cell, recv_param):
    depth_x = field_e.shape[1]
    depth_y = field_e.shape[2]
    sources = recv_param.shape[2]
    capacity = recv_param.shape[3]
    n_x = lax.axis_size("slab") * depth_x
    n_y = lax.axis_size("yz") * depth_y
    stack = jnp.concatenate([field_e, field_h, permittivity, conductivity[None]], 0)
    stack = with_halo(stack, depth_x, depth_y)
    field_e, field_h = stack[0:3], stack[3:6]
    gx = lax.axis_index("slab") * depth_x - HALO + lax.broadcasted_iota(jnp.int32, (1, depth_x + 2 * HALO, 1, 1), 1)
    gy = lax.axis_index("yz") * depth_y - HALO + lax.broadcasted_iota(jnp.int32, (1, 1, depth_y + 2 * HALO, 1), 2)
    inside = (gx >= 0) & (gx < n_x) & (gy >= 0) & (gy < n_y)
    permittivity = jnp.where(inside, stack[6:9], 1.0)
    conductivity = stack[9:10]
    ratio = 0.5 * conductivity / permittivity
    keep_rate = (1.0 - ratio) / (1.0 + ratio)
    curl_gain = CE_GAIN / (permittivity * (1.0 + ratio))
    local = (slice(None), slice(HALO, HALO + depth_x), slice(HALO, HALO + depth_y))
    picked_steps = []
    for step_index in range(STEPS):
        field_h = jnp.where(inside, field_h - CH_GAIN * curl_ahead(field_e), 0.0)
        field_e = jnp.where(inside, keep_rate * field_e + curl_gain * curl_behind(field_h), 0.0)
        picked_steps.append(field_e[local].reshape(3, -1))
    flattened = jnp.stack(picked_steps)
    flattened = jnp.concatenate([flattened, jnp.zeros((STEPS, 3, 1), jnp.float32)], 2)
    picked = jnp.take(flattened, slot_cell.reshape(-1), axis=2)
    products = jnp.sum(picked * forward_e[0, 0], axis=1)
    products = products.reshape(STEPS, sources, capacity).transpose(1, 0, 2)
    received = lax.all_to_all(products, "slab", split_axis=0, concat_axis=0, tiled=True)
    segments = jnp.broadcast_to(recv_param.reshape(sources, 1, capacity), (sources, STEPS, capacity))
    gradient = jax.ops.segment_sum(received.reshape(-1), segments.reshape(-1), num_segments=PAR_DEV + 1)
    return (field_e[local], field_h[local], gradient[:PAR_DEV].reshape(1, 1, PAR_DEV))


def solution(mesh):
    return jax.shard_map(
        shards,
        mesh=mesh,
        in_specs=(
            P(None, "slab", "yz", None),
            P(None, "slab", "yz", None),
            P(None, "slab", "yz", None),
            P("slab", "yz", None),
            P("slab", "yz", None, None, None),
            P("slab", "yz", None, None),
            P("slab", "yz", None, None),
        ),
        out_specs=(P(None, "slab", "yz", None), P(None, "slab", "yz", None), P("slab", "yz", None)),
        check_vma=False,
    )
```

```python
import functools

import jax
import jax.numpy as jnp
from jax import lax
from jax.experimental import pallas as pl
from jax.experimental.pallas import tpu as pltpu
from jax.sharding import PartitionSpec as P

STEPS = 2
PAR_DEV = 128
HALO = 2
LANES = 128

CH_GAIN = 0.5
CE_GAIN = 0.5


def recv_from(array, axis, offset):
    count = lax.axis_size(axis)
    pairs = [(i + offset, i) for i in range(count) if 0 <= i + offset < count]
    return lax.ppermute(array, axis, pairs)


def ahead(values, axis):
    extent = values.shape[axis]
    if axis == 0:
        return jnp.concatenate([values[1:], values[:1]], 0)
    shifted = pltpu.roll(values, extent - 1, axis)
    if axis == 2:
        lane = lax.broadcasted_iota(jnp.int32, values.shape, 2)
        shifted = jnp.where(lane == extent - 1, 0.0, shifted)
    return shifted


def behind(values, axis):
    extent = values.shape[axis]
    if axis == 0:
        return jnp.concatenate([values[extent - 1 :], values[: extent - 1]], 0)
    shifted = pltpu.roll(values, 1, axis)
    if axis == 2:
        lane = lax.broadcasted_iota(jnp.int32, values.shape, 2)
        shifted = jnp.where(lane == 0, 0.0, shifted)
    return shifted


def leapfrog_kernel(
    dims, offsets, e_ref, h_ref, perm_ref, cond_ref, xlo_ref, xhi_ref, ylo_ref, yhi_ref,
    cell_ref, fwd_ref, e_out, h_out, prod_out, ring,
):
    depth_x, depth_y, n_x, n_y = dims
    ring_x, ring_y = ring.shape[1], ring.shape[2]
    ring[0:3, 0:depth_x, 0:depth_y] = e_ref[...]
    ring[3:6, 0:depth_x, 0:depth_y] = h_ref[...]
    ring[6:9, 0:depth_x, 0:depth_y] = perm_ref[...]
    ring[9:10, 0:depth_x, 0:depth_y] = cond_ref[...]
    ring[:, depth_x : depth_x + HALO, 0:depth_y] = xhi_ref[...]
    ring[:, ring_x - HALO : ring_x, 0:depth_y] = xlo_ref[...]
    ring[:, :, depth_y : depth_y + HALO] = yhi_ref[...]
    ring[:, :, depth_y + HALO : ring_y - HALO] = jnp.zeros(
        (ring.shape[0], ring_x, ring_y - depth_y - 2 * HALO, LANES), jnp.float32
    )
    ring[:, :, ring_y - HALO : ring_y] = ylo_ref[...]

    shape = (ring_x, ring_y, LANES)
    xi = lax.broadcasted_iota(jnp.int32, shape, 0)
    yi = lax.broadcasted_iota(jnp.int32, shape, 1)
    gx = offsets[0] + jnp.where(xi < depth_x + HALO, xi, xi - ring_x)
    gy = offsets[1] + jnp.where(yi < depth_y + HALO, yi, yi - ring_y)
    y_real = (yi < depth_y + HALO) | (yi >= ring_y - HALO)
    inside = (gx >= 0) & (gx < n_x) & (gy >= 0) & (gy < n_y) & y_real

    field_e = [ring[c] for c in range(3)]
    field_h = [ring[3 + c] for c in range(3)]
    conductivity = ring[9]
    keep_rate, curl_gain = [], []
    for c in range(3):
        permittivity = jnp.where(inside, ring[6 + c], 1.0)
        ratio = 0.5 * conductivity / permittivity
        keep_rate.append((1.0 - ratio) / (1.0 + ratio))
        curl_gain.append(CE_GAIN / (permittivity * (1.0 + ratio)))

    cells = cell_ref[...]
    rows = depth_x * depth_y
    lane_pick = (lax.broadcasted_iota(jnp.int32, (LANES, cells.shape[1]), 0) == (cells % LANES)).astype(jnp.float32)
    row_pick = lax.broadcasted_iota(jnp.int32, (rows, cells.shape[1]), 0) == (cells // LANES)

    for step_index in range(STEPS):
        e0, e1, e2 = field_e
        curl = (
            (ahead(e2, 1) - e2) - (ahead(e1, 2) - e1),
            (ahead(e0, 2) - e0) - (ahead(e2, 0) - e2),
            (ahead(e1, 0) - e1) - (ahead(e0, 1) - e0),
        )
        field_h = [jnp.where(inside, field_h[c] - CH_GAIN * curl[c], 0.0) for c in range(3)]
        h0, h1, h2 = field_h
        curl = (
            (h2 - behind(h2, 1)) - (h1 - behind(h1, 2)),
            (h0 - behind(h0, 2)) - (h2 - behind(h2, 0)),
            (h1 - behind(h1, 0)) - (h0 - behind(h0, 1)),
        )
        field_e = [
            jnp.where(inside, keep_rate[c] * field_e[c] + curl_gain[c] * curl[c], 0.0) for c in range(3)
        ]
        product = None
        for c in range(3):
            block = field_e[c][0:depth_x, 0:depth_y].reshape(rows, LANES)
            by_lane = jnp.dot(block, lane_pick, precision=lax.Precision.HIGHEST, preferred_element_type=jnp.float32)
            picked = jnp.sum(jnp.where(row_pick, by_lane, 0.0), axis=0, keepdims=True)
            term = picked * fwd_ref[step_index, c : c + 1, :]
            product = term if product is None else product + term
        prod_out[step_index : step_index + 1, :] = product

    for c in range(3):
        e_out[c] = field_e[c][0:depth_x, 0:depth_y]
        h_out[c] = field_h[c][0:depth_x, 0:depth_y]


def leapfrog(offsets, field_e, field_h, permittivity, conductivity, xlo, xhi, ylo, yhi, cells, fwd, n_x, n_y):
    _, depth_x, depth_y, _ = field_e.shape
    ring_x = depth_x + 2 * HALO
    ring_y = -(-(depth_y + 2 * HALO) // 8) * 8
    vmem = pl.BlockSpec(memory_space=pltpu.VMEM)
    smem = pl.BlockSpec(memory_space=pltpu.SMEM)
    kernel = functools.partial(leapfrog_kernel, (depth_x, depth_y, n_x, n_y))
    return pl.pallas_call(
        kernel,
        out_shape=(
            jax.ShapeDtypeStruct(field_e.shape, jnp.float32),
            jax.ShapeDtypeStruct(field_h.shape, jnp.float32),
            jax.ShapeDtypeStruct((STEPS, cells.shape[1]), jnp.float32),
        ),
        in_specs=[smem] + [vmem] * 10,
        out_specs=(vmem, vmem, vmem),
        scratch_shapes=[pltpu.VMEM((10, ring_x, ring_y, LANES), jnp.float32)],
    )(offsets, field_e, field_h, permittivity, conductivity, xlo, xhi, ylo, yhi, cells, fwd)


def shards(field_e, field_h, permittivity, conductivity, forward_e, slot_cell, recv_param):
    depth_x = field_e.shape[1]
    depth_y = field_e.shape[2]
    sources = recv_param.shape[2]
    capacity = recv_param.shape[3]
    n_x = lax.axis_size("slab") * depth_x
    n_y = lax.axis_size("yz") * depth_y
    parts = (field_e, field_h, permittivity, conductivity[None])
    xlo = recv_from(jnp.concatenate([p[:, depth_x - HALO :] for p in parts], 0), "slab", -1)
    xhi = recv_from(jnp.concatenate([p[:, :HALO] for p in parts], 0), "slab", 1)
    def rows(start):
        center = jnp.concatenate([p[:, :, start : start + HALO] for p in parts], 0)
        return jnp.concatenate([center, xhi[:, :, start : start + HALO], xlo[:, :, start : start + HALO]], 1)

    ylo = recv_from(rows(depth_y - HALO), "yz", -1)
    yhi = recv_from(rows(0), "yz", 1)
    offsets = jnp.stack([lax.axis_index("slab") * depth_x, lax.axis_index("yz") * depth_y]).astype(jnp.int32)
    new_e, new_h, products = leapfrog(
        offsets, field_e, field_h, permittivity, conductivity[None], xlo, xhi, ylo, yhi,
        slot_cell.reshape(1, -1), forward_e[0, 0], n_x, n_y,
    )
    products = products.reshape(STEPS, sources, capacity)
    received = lax.all_to_all(products, "slab", split_axis=1, concat_axis=1, tiled=True)
    segments = jnp.broadcast_to(recv_param.reshape(1, sources, capacity), (STEPS, sources, capacity))
    gradient = jax.ops.segment_sum(received.reshape(-1), segments.reshape(-1), num_segments=PAR_DEV + 1)
    return (new_e, new_h, gradient[:PAR_DEV].reshape(1, 1, PAR_DEV))


def solution(mesh):
    return jax.shard_map(
        shards,
        mesh=mesh,
        in_specs=(
            P(None, "slab", "yz", None),
            P(None, "slab", "yz", None),
            P(None, "slab", "yz", None),
            P("slab", "yz", None),
            P("slab", "yz", None, None, None),
            P("slab", "yz", None, None),
            P("slab", "yz", None, None),
        ),
        out_specs=(P(None, "slab", "yz", None), P(None, "slab", "yz", None), P("slab", "yz", None)),
        check_vma=False,
    )
```

```python
import functools

import jax
import jax.numpy as jnp
from jax import lax
from jax.experimental import pallas as pl
from jax.experimental.pallas import tpu as pltpu
from jax.sharding import PartitionSpec as P

STEPS = 2
PAR_DEV = 128
HALO = 2
LANES = 128
MAX_PERMUTE_RING = 8

CH_GAIN = 0.5
CE_GAIN = 0.5


def recv_from(array, axis, offset):
    count = lax.axis_size(axis)
    pairs = [(i + offset, i) for i in range(count) if 0 <= i + offset < count]
    return lax.ppermute(array, axis, pairs)


def ahead(values, axis):
    extent = values.shape[axis]
    if axis == 0:
        return jnp.concatenate([values[1:], values[:1]], 0)
    shifted = pltpu.roll(values, extent - 1, axis)
    if axis == 2:
        lane = lax.broadcasted_iota(jnp.int32, values.shape, 2)
        shifted = jnp.where(lane == extent - 1, 0.0, shifted)
    return shifted


def behind(values, axis):
    extent = values.shape[axis]
    if axis == 0:
        return jnp.concatenate([values[extent - 1 :], values[: extent - 1]], 0)
    shifted = pltpu.roll(values, 1, axis)
    if axis == 2:
        lane = lax.broadcasted_iota(jnp.int32, values.shape, 2)
        shifted = jnp.where(lane == 0, 0.0, shifted)
    return shifted


def leapfrog_kernel(
    dims, offsets, e_ref, h_ref, perm_ref, cond_ref, xlo_ref, xhi_ref, ylo_ref, yhi_ref,
    cell_ref, fwd_ref, e_out, h_out, prod_out, ring,
):
    depth_x, depth_y, n_x, n_y = dims
    ring_x, ring_y = ring.shape[1], ring.shape[2]
    ring[0:3, 0:depth_x, 0:depth_y] = e_ref[...]
    ring[3:6, 0:depth_x, 0:depth_y] = h_ref[...]
    ring[6:9, 0:depth_x, 0:depth_y] = perm_ref[...]
    ring[9:10, 0:depth_x, 0:depth_y] = cond_ref[...]
    ring[:, depth_x : depth_x + HALO, 0:depth_y] = xhi_ref[...]
    ring[:, ring_x - HALO : ring_x, 0:depth_y] = xlo_ref[...]
    ring[:, :, depth_y : depth_y + HALO] = yhi_ref[...]
    ring[:, :, depth_y + HALO : ring_y - HALO] = jnp.zeros(
        (ring.shape[0], ring_x, ring_y - depth_y - 2 * HALO, LANES), jnp.float32
    )
    ring[:, :, ring_y - HALO : ring_y] = ylo_ref[...]

    shape = (ring_x, ring_y, LANES)
    xi = lax.broadcasted_iota(jnp.int32, shape, 0)
    yi = lax.broadcasted_iota(jnp.int32, shape, 1)
    gx = offsets[0] + jnp.where(xi < depth_x + HALO, xi, xi - ring_x)
    gy = offsets[1] + jnp.where(yi < depth_y + HALO, yi, yi - ring_y)
    y_real = (yi < depth_y + HALO) | (yi >= ring_y - HALO)
    inside = (gx >= 0) & (gx < n_x) & (gy >= 0) & (gy < n_y) & y_real

    field_e = [ring[c] for c in range(3)]
    field_h = [ring[3 + c] for c in range(3)]
    conductivity = ring[9]
    keep_rate, curl_gain = [], []
    for c in range(3):
        permittivity = jnp.where(inside, ring[6 + c], 1.0)
        ratio = 0.5 * conductivity / permittivity
        keep_rate.append((1.0 - ratio) / (1.0 + ratio))
        curl_gain.append(CE_GAIN / (permittivity * (1.0 + ratio)))

    cells = cell_ref[...]
    rows = depth_x * depth_y
    lane_pick = (lax.broadcasted_iota(jnp.int32, (LANES, cells.shape[1]), 0) == (cells % LANES)).astype(jnp.float32)
    row_pick = lax.broadcasted_iota(jnp.int32, (rows, cells.shape[1]), 0) == (cells // LANES)

    for step_index in range(STEPS):
        e0, e1, e2 = field_e
        curl = (
            (ahead(e2, 1) - e2) - (ahead(e1, 2) - e1),
            (ahead(e0, 2) - e0) - (ahead(e2, 0) - e2),
            (ahead(e1, 0) - e1) - (ahead(e0, 1) - e0),
        )
        field_h = [jnp.where(inside, field_h[c] - CH_GAIN * curl[c], 0.0) for c in range(3)]
        h0, h1, h2 = field_h
        curl = (
            (h2 - behind(h2, 1)) - (h1 - behind(h1, 2)),
            (h0 - behind(h0, 2)) - (h2 - behind(h2, 0)),
            (h1 - behind(h1, 0)) - (h0 - behind(h0, 1)),
        )
        field_e = [
            jnp.where(inside, keep_rate[c] * field_e[c] + curl_gain[c] * curl[c], 0.0) for c in range(3)
        ]
        product = None
        for c in range(3):
            block = field_e[c][0:depth_x, 0:depth_y].reshape(rows, LANES)
            by_lane = jnp.dot(block, lane_pick, precision=lax.Precision.HIGHEST, preferred_element_type=jnp.float32)
            picked = jnp.sum(jnp.where(row_pick, by_lane, 0.0), axis=0, keepdims=True)
            term = picked * fwd_ref[step_index, c : c + 1, :]
            product = term if product is None else product + term
        prod_out[step_index : step_index + 1, :] = product

    for c in range(3):
        e_out[c] = field_e[c][0:depth_x, 0:depth_y]
        h_out[c] = field_h[c][0:depth_x, 0:depth_y]


def leapfrog(offsets, field_e, field_h, permittivity, conductivity, xlo, xhi, ylo, yhi, cells, fwd, n_x, n_y):
    _, depth_x, depth_y, _ = field_e.shape
    ring_x = depth_x + 2 * HALO
    ring_y = -(-(depth_y + 2 * HALO) // 8) * 8
    vmem = pl.BlockSpec(memory_space=pltpu.VMEM)
    smem = pl.BlockSpec(memory_space=pltpu.SMEM)
    kernel = functools.partial(leapfrog_kernel, (depth_x, depth_y, n_x, n_y))
    return pl.pallas_call(
        kernel,
        out_shape=(
            jax.ShapeDtypeStruct(field_e.shape, jnp.float32),
            jax.ShapeDtypeStruct(field_h.shape, jnp.float32),
            jax.ShapeDtypeStruct((STEPS, cells.shape[1]), jnp.float32),
        ),
        in_specs=[smem] + [vmem] * 10,
        out_specs=(vmem, vmem, vmem),
        scratch_shapes=[pltpu.VMEM((10, ring_x, ring_y, LANES), jnp.float32)],
    )(offsets, field_e, field_h, permittivity, conductivity, xlo, xhi, ylo, yhi, cells, fwd)


def exchange_by_permutes(products, segments, count):
    me = lax.axis_index("slab")
    doubled = jnp.concatenate([products, products], 1)
    rotated = lax.dynamic_slice_in_dim(doubled, me, count, axis=1)
    pieces = [rotated[:, 0]]
    for shift in range(1, count):
        pairs = [(i, (i + shift) % count) for i in range(count)]
        pieces.append(lax.ppermute(rotated[:, shift], "slab", pairs))
    received = jnp.stack(pieces, 1)
    backwards = segments[::-1]
    doubled = jnp.concatenate([backwards, backwards], 0)
    sources = lax.dynamic_slice_in_dim(doubled, count - 1 - me, count, axis=0)
    return received, sources


def shards(field_e, field_h, permittivity, conductivity, forward_e, slot_cell, recv_param):
    depth_x = field_e.shape[1]
    depth_y = field_e.shape[2]
    sources = recv_param.shape[2]
    capacity = recv_param.shape[3]
    n_x = lax.axis_size("slab") * depth_x
    n_y = lax.axis_size("yz") * depth_y
    parts = (field_e, field_h, permittivity, conductivity[None])
    xlo = recv_from(jnp.concatenate([p[:, depth_x - HALO :] for p in parts], 0), "slab", -1)
    xhi = recv_from(jnp.concatenate([p[:, :HALO] for p in parts], 0), "slab", 1)
    def rows(start):
        center = jnp.concatenate([p[:, :, start : start + HALO] for p in parts], 0)
        return jnp.concatenate([center, xhi[:, :, start : start + HALO], xlo[:, :, start : start + HALO]], 1)

    ylo = recv_from(rows(depth_y - HALO), "yz", -1)
    yhi = recv_from(rows(0), "yz", 1)
    offsets = jnp.stack([lax.axis_index("slab") * depth_x, lax.axis_index("yz") * depth_y]).astype(jnp.int32)
    new_e, new_h, products = leapfrog(
        offsets, field_e, field_h, permittivity, conductivity[None], xlo, xhi, ylo, yhi,
        slot_cell.reshape(1, -1), forward_e[0, 0], n_x, n_y,
    )
    products = products.reshape(STEPS, sources, capacity)
    segments = recv_param.reshape(sources, capacity)
    if sources <= MAX_PERMUTE_RING:
        received, segments = exchange_by_permutes(products, segments, sources)
    else:
        received = lax.all_to_all(products, "slab", split_axis=1, concat_axis=1, tiled=True)
    segments = jnp.broadcast_to(segments[None], (STEPS, sources, capacity))
    gradient = jax.ops.segment_sum(received.reshape(-1), segments.reshape(-1), num_segments=PAR_DEV + 1)
    return (new_e, new_h, gradient[:PAR_DEV].reshape(1, 1, PAR_DEV))


def solution(mesh):
    return jax.shard_map(
        shards,
        mesh=mesh,
        in_specs=(
            P(None, "slab", "yz", None),
            P(None, "slab", "yz", None),
            P(None, "slab", "yz", None),
            P("slab", "yz", None),
            P("slab", "yz", None, None, None),
            P("slab", "yz", None, None),
            P("slab", "yz", None, None),
        ),
        out_specs=(P(None, "slab", "yz", None), P(None, "slab", "yz", None), P("slab", "yz", None)),
        check_vma=False,
    )
```

```python
import functools

import jax
import jax.numpy as jnp
from jax import lax
from jax.experimental import pallas as pl
from jax.experimental.pallas import tpu as pltpu
from jax.sharding import PartitionSpec as P

STEPS = 2
PAR_DEV = 128
HALO = 2
LANES = 128

CH_GAIN = 0.5
CE_GAIN = 0.5


def recv_from(array, axis, offset):
    count = lax.axis_size(axis)
    pairs = [(i + offset, i) for i in range(count) if 0 <= i + offset < count]
    return lax.ppermute(array, axis, pairs)


def ahead(values, axis):
    extent = values.shape[axis]
    if axis == 0:
        return jnp.concatenate([values[1:], values[:1]], 0)
    shifted = pltpu.roll(values, extent - 1, axis)
    if axis == 2:
        lane = lax.broadcasted_iota(jnp.int32, values.shape, 2)
        shifted = jnp.where(lane == extent - 1, 0.0, shifted)
    return shifted


def behind(values, axis):
    extent = values.shape[axis]
    if axis == 0:
        return jnp.concatenate([values[extent - 1 :], values[: extent - 1]], 0)
    shifted = pltpu.roll(values, 1, axis)
    if axis == 2:
        lane = lax.broadcasted_iota(jnp.int32, values.shape, 2)
        shifted = jnp.where(lane == 0, 0.0, shifted)
    return shifted


def leapfrog_kernel(
    dims, offsets, e_ref, h_ref, perm_ref, cond_ref, xlo_ref, xhi_ref, ylo_ref, yhi_ref,
    cell_ref, fwd_ref, e_out, h_out, prod_out, ring,
):
    depth_x, depth_y, n_x, n_y = dims
    ring_x, ring_y = ring.shape[1], ring.shape[2]
    ring[0:3, 0:depth_x, 0:depth_y] = e_ref[...]
    ring[3:6, 0:depth_x, 0:depth_y] = h_ref[...]
    ring[6:9, 0:depth_x, 0:depth_y] = perm_ref[...]
    ring[9:10, 0:depth_x, 0:depth_y] = cond_ref[...]
    ring[:, depth_x : depth_x + HALO, 0:depth_y] = xhi_ref[...]
    ring[:, ring_x - HALO : ring_x, 0:depth_y] = xlo_ref[...]
    ring[:, :, depth_y : depth_y + HALO] = yhi_ref[...]
    ring[:, :, depth_y + HALO : ring_y - HALO] = jnp.zeros(
        (ring.shape[0], ring_x, ring_y - depth_y - 2 * HALO, LANES), jnp.float32
    )
    ring[:, :, ring_y - HALO : ring_y] = ylo_ref[...]

    shape = (ring_x, ring_y, LANES)
    xi = lax.broadcasted_iota(jnp.int32, shape, 0)
    yi = lax.broadcasted_iota(jnp.int32, shape, 1)
    gx = offsets[0] + jnp.where(xi < depth_x + HALO, xi, xi - ring_x)
    gy = offsets[1] + jnp.where(yi < depth_y + HALO, yi, yi - ring_y)
    y_real = (yi < depth_y + HALO) | (yi >= ring_y - HALO)
    inside = (gx >= 0) & (gx < n_x) & (gy >= 0) & (gy < n_y) & y_real

    field_e = [ring[c] for c in range(3)]
    field_h = [ring[3 + c] for c in range(3)]
    conductivity = ring[9]
    keep_rate, curl_gain = [], []
    for c in range(3):
        permittivity = jnp.where(inside, ring[6 + c], 1.0)
        ratio = 0.5 * conductivity / permittivity
        keep_rate.append((1.0 - ratio) / (1.0 + ratio))
        curl_gain.append(CE_GAIN / (permittivity * (1.0 + ratio)))

    cells = cell_ref[...]
    rows = depth_x * depth_y
    lane_pick = (lax.broadcasted_iota(jnp.int32, (LANES, cells.shape[1]), 0) == (cells % LANES)).astype(jnp.float32)
    row_pick = lax.broadcasted_iota(jnp.int32, (rows, cells.shape[1]), 0) == (cells // LANES)

    for step_index in range(STEPS):
        e0, e1, e2 = field_e
        curl = (
            (ahead(e2, 1) - e2) - (ahead(e1, 2) - e1),
            (ahead(e0, 2) - e0) - (ahead(e2, 0) - e2),
            (ahead(e1, 0) - e1) - (ahead(e0, 1) - e0),
        )
        field_h = [jnp.where(inside, field_h[c] - CH_GAIN * curl[c], 0.0) for c in range(3)]
        h0, h1, h2 = field_h
        curl = (
            (h2 - behind(h2, 1)) - (h1 - behind(h1, 2)),
            (h0 - behind(h0, 2)) - (h2 - behind(h2, 0)),
            (h1 - behind(h1, 0)) - (h0 - behind(h0, 1)),
        )
        field_e = [
            jnp.where(inside, keep_rate[c] * field_e[c] + curl_gain[c] * curl[c], 0.0) for c in range(3)
        ]
        product = None
        for c in range(3):
            block = field_e[c][0:depth_x, 0:depth_y].reshape(rows, LANES)
            by_lane = jnp.dot(block, lane_pick, precision=lax.Precision.HIGHEST, preferred_element_type=jnp.float32)
            picked = jnp.sum(jnp.where(row_pick, by_lane, 0.0), axis=0, keepdims=True)
            term = picked * fwd_ref[step_index, c : c + 1, :]
            product = term if product is None else product + term
        prod_out[step_index : step_index + 1, :] = product

    for c in range(3):
        e_out[c] = field_e[c][0:depth_x, 0:depth_y]
        h_out[c] = field_h[c][0:depth_x, 0:depth_y]


def leapfrog(offsets, field_e, field_h, permittivity, conductivity, xlo, xhi, ylo, yhi, cells, fwd, n_x, n_y):
    _, depth_x, depth_y, _ = field_e.shape
    ring_x = depth_x + 2 * HALO
    ring_y = -(-(depth_y + 2 * HALO) // 8) * 8
    vmem = pl.BlockSpec(memory_space=pltpu.VMEM)
    smem = pl.BlockSpec(memory_space=pltpu.SMEM)
    kernel = functools.partial(leapfrog_kernel, (depth_x, depth_y, n_x, n_y))
    return pl.pallas_call(
        kernel,
        out_shape=(
            jax.ShapeDtypeStruct(field_e.shape, jnp.float32),
            jax.ShapeDtypeStruct(field_h.shape, jnp.float32),
            jax.ShapeDtypeStruct((STEPS, cells.shape[1]), jnp.float32),
        ),
        in_specs=[smem] + [vmem] * 10,
        out_specs=(vmem, vmem, vmem),
        scratch_shapes=[pltpu.VMEM((10, ring_x, ring_y, LANES), jnp.float32)],
    )(offsets, field_e, field_h, permittivity, conductivity, xlo, xhi, ylo, yhi, cells, fwd)


def xor_rows(array, me, count, axis):
    bit = 1
    while bit < count:
        shape = array.shape[:axis] + (count // (2 * bit), 2, bit) + array.shape[axis + 1 :]
        split = array.reshape(shape)
        swapped = jnp.flip(split, axis + 1).reshape(array.shape)
        array = jnp.where((me // bit) % 2 == 1, swapped, array)
        bit *= 2
    return array


def exchange_by_halving(products, segments, count):
    me = lax.axis_index("slab")
    held = xor_rows(products, me, count, 1)[:, :, None]
    bit = count // 2
    while bit >= 1:
        owners = held.shape[1]
        keep = held[:, : owners // 2]
        send = held[:, owners // 2 :]
        pairs = [(i, i ^ bit) for i in range(count)]
        got = lax.ppermute(send, "slab", pairs)
        held = jnp.stack([keep, got], 3).reshape(keep.shape[:2] + (keep.shape[2] * 2,) + keep.shape[3:])
        bit //= 2
    return held[:, 0], xor_rows(segments, me, count, 0)


def shards(field_e, field_h, permittivity, conductivity, forward_e, slot_cell, recv_param):
    depth_x = field_e.shape[1]
    depth_y = field_e.shape[2]
    sources = recv_param.shape[2]
    capacity = recv_param.shape[3]
    n_x = lax.axis_size("slab") * depth_x
    n_y = lax.axis_size("yz") * depth_y
    parts = (field_e, field_h, permittivity, conductivity[None])
    xlo = recv_from(jnp.concatenate([p[:, depth_x - HALO :] for p in parts], 0), "slab", -1)
    xhi = recv_from(jnp.concatenate([p[:, :HALO] for p in parts], 0), "slab", 1)
    def rows(start):
        center = jnp.concatenate([p[:, :, start : start + HALO] for p in parts], 0)
        return jnp.concatenate([center, xhi[:, :, start : start + HALO], xlo[:, :, start : start + HALO]], 1)

    ylo = recv_from(rows(depth_y - HALO), "yz", -1)
    yhi = recv_from(rows(0), "yz", 1)
    offsets = jnp.stack([lax.axis_index("slab") * depth_x, lax.axis_index("yz") * depth_y]).astype(jnp.int32)
    new_e, new_h, products = leapfrog(
        offsets, field_e, field_h, permittivity, conductivity[None], xlo, xhi, ylo, yhi,
        slot_cell.reshape(1, -1), forward_e[0, 0], n_x, n_y,
    )
    products = products.reshape(STEPS, sources, capacity)
    segments = recv_param.reshape(sources, capacity)
    if sources & (sources - 1) == 0:
        received, segments = exchange_by_halving(products, segments, sources)
    else:
        received = lax.all_to_all(products, "slab", split_axis=1, concat_axis=1, tiled=True)
    segments = jnp.broadcast_to(segments[None], received.shape)
    gradient = jax.ops.segment_sum(received.reshape(-1), segments.reshape(-1), num_segments=PAR_DEV + 1)
    return (new_e, new_h, gradient[:PAR_DEV].reshape(1, 1, PAR_DEV))


def solution(mesh):
    return jax.shard_map(
        shards,
        mesh=mesh,
        in_specs=(
            P(None, "slab", "yz", None),
            P(None, "slab", "yz", None),
            P(None, "slab", "yz", None),
            P("slab", "yz", None),
            P("slab", "yz", None, None, None),
            P("slab", "yz", None, None),
            P("slab", "yz", None, None),
        ),
        out_specs=(P(None, "slab", "yz", None), P(None, "slab", "yz", None), P("slab", "yz", None)),
        check_vma=False,
    )
```

```python
import functools

import jax
import jax.numpy as jnp
from jax import lax
from jax.experimental import pallas as pl
from jax.experimental.pallas import tpu as pltpu
from jax.sharding import PartitionSpec as P

STEPS = 2
PAR_DEV = 128
HALO = 2
LANES = 128

CH_GAIN = 0.5
CE_GAIN = 0.5


def recv_from(array, axis, offset):
    count = lax.axis_size(axis)
    pairs = [(i + offset, i) for i in range(count) if 0 <= i + offset < count]
    return lax.ppermute(array, axis, pairs)


def ahead(values, axis):
    extent = values.shape[axis]
    if axis == 0:
        return jnp.concatenate([values[1:], values[:1]], 0)
    shifted = pltpu.roll(values, extent - 1, axis)
    if axis == 2:
        lane = lax.broadcasted_iota(jnp.int32, values.shape, 2)
        shifted = jnp.where(lane == extent - 1, 0.0, shifted)
    return shifted


def behind(values, axis):
    extent = values.shape[axis]
    if axis == 0:
        return jnp.concatenate([values[extent - 1 :], values[: extent - 1]], 0)
    shifted = pltpu.roll(values, 1, axis)
    if axis == 2:
        lane = lax.broadcasted_iota(jnp.int32, values.shape, 2)
        shifted = jnp.where(lane == 0, 0.0, shifted)
    return shifted


def leapfrog_kernel(
    dims, offsets, e_ref, h_ref, perm_ref, cond_ref, xlo_ref, xhi_ref, ylo_ref, yhi_ref,
    cell_ref, fwd_ref, e_out, h_out, prod_out, ring, *staged,
):
    sources = (e_ref, h_ref, perm_ref, cond_ref, xlo_ref, xhi_ref, ylo_ref, yhi_ref, cell_ref, fwd_ref)
    buffers, sems = staged[:-1], staged[-1]
    copies = [pltpu.make_async_copy(src, buf, sems.at[i]) for i, (src, buf) in enumerate(zip(sources, buffers))]
    for copy in copies:
        copy.start()
    for copy in copies:
        copy.wait()
    e_ref, h_ref, perm_ref, cond_ref, xlo_ref, xhi_ref, ylo_ref, yhi_ref, cell_ref, fwd_ref = buffers
    depth_x, depth_y, n_x, n_y = dims
    ring_x, ring_y = ring.shape[1], ring.shape[2]
    ring[0:3, 0:depth_x, 0:depth_y] = e_ref[...]
    ring[3:6, 0:depth_x, 0:depth_y] = h_ref[...]
    ring[6:9, 0:depth_x, 0:depth_y] = perm_ref[...]
    ring[9:10, 0:depth_x, 0:depth_y] = cond_ref[...]
    ring[:, depth_x : depth_x + HALO, 0:depth_y] = xhi_ref[...]
    ring[:, ring_x - HALO : ring_x, 0:depth_y] = xlo_ref[...]
    ring[:, :, depth_y : depth_y + HALO] = yhi_ref[...]
    ring[:, :, depth_y + HALO : ring_y - HALO] = jnp.zeros(
        (ring.shape[0], ring_x, ring_y - depth_y - 2 * HALO, LANES), jnp.float32
    )
    ring[:, :, ring_y - HALO : ring_y] = ylo_ref[...]

    shape = (ring_x, ring_y, LANES)
    xi = lax.broadcasted_iota(jnp.int32, shape, 0)
    yi = lax.broadcasted_iota(jnp.int32, shape, 1)
    gx = offsets[0] + jnp.where(xi < depth_x + HALO, xi, xi - ring_x)
    gy = offsets[1] + jnp.where(yi < depth_y + HALO, yi, yi - ring_y)
    y_real = (yi < depth_y + HALO) | (yi >= ring_y - HALO)
    inside = (gx >= 0) & (gx < n_x) & (gy >= 0) & (gy < n_y) & y_real

    field_e = [ring[c] for c in range(3)]
    field_h = [ring[3 + c] for c in range(3)]
    conductivity = ring[9]
    keep_rate, curl_gain = [], []
    for c in range(3):
        permittivity = jnp.where(inside, ring[6 + c], 1.0)
        ratio = 0.5 * conductivity / permittivity
        keep_rate.append((1.0 - ratio) / (1.0 + ratio))
        curl_gain.append(CE_GAIN / (permittivity * (1.0 + ratio)))

    cells = cell_ref[...]
    rows = depth_x * depth_y
    lane_pick = (lax.broadcasted_iota(jnp.int32, (LANES, cells.shape[1]), 0) == (cells % LANES)).astype(jnp.float32)
    row_pick = lax.broadcasted_iota(jnp.int32, (rows, cells.shape[1]), 0) == (cells // LANES)

    for step_index in range(STEPS):
        e0, e1, e2 = field_e
        curl = (
            (ahead(e2, 1) - e2) - (ahead(e1, 2) - e1),
            (ahead(e0, 2) - e0) - (ahead(e2, 0) - e2),
            (ahead(e1, 0) - e1) - (ahead(e0, 1) - e0),
        )
        field_h = [jnp.where(inside, field_h[c] - CH_GAIN * curl[c], 0.0) for c in range(3)]
        h0, h1, h2 = field_h
        curl = (
            (h2 - behind(h2, 1)) - (h1 - behind(h1, 2)),
            (h0 - behind(h0, 2)) - (h2 - behind(h2, 0)),
            (h1 - behind(h1, 0)) - (h0 - behind(h0, 1)),
        )
        field_e = [
            jnp.where(inside, keep_rate[c] * field_e[c] + curl_gain[c] * curl[c], 0.0) for c in range(3)
        ]
        product = None
        for c in range(3):
            block = field_e[c][0:depth_x, 0:depth_y].reshape(rows, LANES)
            by_lane = jnp.dot(block, lane_pick, precision=lax.Precision.HIGHEST, preferred_element_type=jnp.float32)
            picked = jnp.sum(jnp.where(row_pick, by_lane, 0.0), axis=0, keepdims=True)
            term = picked * fwd_ref[step_index, c : c + 1, :]
            product = term if product is None else product + term
        prod_out[step_index : step_index + 1, :] = product

    for c in range(3):
        e_out[c] = field_e[c][0:depth_x, 0:depth_y]
        h_out[c] = field_h[c][0:depth_x, 0:depth_y]


def leapfrog(offsets, field_e, field_h, permittivity, conductivity, xlo, xhi, ylo, yhi, cells, fwd, n_x, n_y):
    _, depth_x, depth_y, _ = field_e.shape
    ring_x = depth_x + 2 * HALO
    ring_y = -(-(depth_y + 2 * HALO) // 8) * 8
    whole = pl.BlockSpec()
    anywhere = pl.BlockSpec(memory_space=pl.ANY)
    operands = (field_e, field_h, permittivity, conductivity, xlo, xhi, ylo, yhi, cells, fwd)
    smem = pl.BlockSpec(memory_space=pltpu.SMEM)
    kernel = functools.partial(leapfrog_kernel, (depth_x, depth_y, n_x, n_y))
    return pl.pallas_call(
        kernel,
        out_shape=(
            jax.ShapeDtypeStruct(field_e.shape, jnp.float32),
            jax.ShapeDtypeStruct(field_h.shape, jnp.float32),
            jax.ShapeDtypeStruct((STEPS, cells.shape[1]), jnp.float32),
        ),
        in_specs=[smem] + [anywhere] * 10,
        out_specs=(whole, whole, whole),
        scratch_shapes=[pltpu.VMEM((10, ring_x, ring_y, LANES), jnp.float32)]
        + [pltpu.VMEM(a.shape, a.dtype) for a in operands]
        + [pltpu.SemaphoreType.DMA((len(operands),))],
    )(offsets, *operands)


def xor_rows(array, me, count, axis):
    bit = 1
    while bit < count:
        shape = array.shape[:axis] + (count // (2 * bit), 2, bit) + array.shape[axis + 1 :]
        split = array.reshape(shape)
        swapped = jnp.flip(split, axis + 1).reshape(array.shape)
        array = jnp.where((me // bit) % 2 == 1, swapped, array)
        bit *= 2
    return array


def exchange_by_halving(products, segments, count):
    me = lax.axis_index("slab")
    held = xor_rows(products, me, count, 1)[:, :, None]
    bit = count // 2
    while bit >= 1:
        owners = held.shape[1]
        keep = held[:, : owners // 2]
        send = held[:, owners // 2 :]
        pairs = [(i, i ^ bit) for i in range(count)]
        got = lax.ppermute(send, "slab", pairs)
        held = jnp.stack([keep, got], 3).reshape(keep.shape[:2] + (keep.shape[2] * 2,) + keep.shape[3:])
        bit //= 2
    return held[:, 0], xor_rows(segments, me, count, 0)


def shards(field_e, field_h, permittivity, conductivity, forward_e, slot_cell, recv_param):
    depth_x = field_e.shape[1]
    depth_y = field_e.shape[2]
    sources = recv_param.shape[2]
    capacity = recv_param.shape[3]
    n_x = lax.axis_size("slab") * depth_x
    n_y = lax.axis_size("yz") * depth_y
    parts = (field_e, field_h, permittivity, conductivity[None])
    xlo = recv_from(jnp.concatenate([p[:, depth_x - HALO :] for p in parts], 0), "slab", -1)
    xhi = recv_from(jnp.concatenate([p[:, :HALO] for p in parts], 0), "slab", 1)
    def rows(start):
        center = jnp.concatenate([p[:, :, start : start + HALO] for p in parts], 0)
        return jnp.concatenate([center, xhi[:, :, start : start + HALO], xlo[:, :, start : start + HALO]], 1)

    ylo = recv_from(rows(depth_y - HALO), "yz", -1)
    yhi = recv_from(rows(0), "yz", 1)
    offsets = jnp.stack([lax.axis_index("slab") * depth_x, lax.axis_index("yz") * depth_y]).astype(jnp.int32)
    new_e, new_h, products = leapfrog(
        offsets, field_e, field_h, permittivity, conductivity[None], xlo, xhi, ylo, yhi,
        slot_cell.reshape(1, -1), forward_e[0, 0], n_x, n_y,
    )
    products = products.reshape(STEPS, sources, capacity)
    segments = recv_param.reshape(sources, capacity)
    if sources & (sources - 1) == 0:
        received, segments = exchange_by_halving(products, segments, sources)
    else:
        received = lax.all_to_all(products, "slab", split_axis=1, concat_axis=1, tiled=True)
    segments = jnp.broadcast_to(segments[None], received.shape).reshape(-1, 1)
    params = lax.broadcasted_iota(jnp.int32, (1, PAR_DEV), 1)
    gradient = jnp.sum(jnp.where(segments == params, received.reshape(-1, 1), 0.0), axis=0)
    return (new_e, new_h, gradient.reshape(1, 1, PAR_DEV))


def solution(mesh):
    return jax.shard_map(
        shards,
        mesh=mesh,
        in_specs=(
            P(None, "slab", "yz", None),
            P(None, "slab", "yz", None),
            P(None, "slab", "yz", None),
            P("slab", "yz", None),
            P("slab", "yz", None, None, None),
            P("slab", "yz", None, None),
            P("slab", "yz", None, None),
        ),
        out_specs=(P(None, "slab", "yz", None), P(None, "slab", "yz", None), P("slab", "yz", None)),
        check_vma=False,
    )
```

```python
import functools

import jax
import jax.numpy as jnp
from jax import lax
from jax.experimental import pallas as pl
from jax.experimental.pallas import tpu as pltpu
from jax.sharding import PartitionSpec as P

STEPS = 2
PAR_DEV = 128
HALO = 2
LANES = 128

CH_GAIN = 0.5
CE_GAIN = 0.5


def recv_from(array, axis, offset):
    count = lax.axis_size(axis)
    pairs = [(i + offset, i) for i in range(count) if 0 <= i + offset < count]
    return lax.ppermute(array, axis, pairs)


def ahead(values, axis):
    extent = values.shape[axis]
    if axis == 0:
        return jnp.concatenate([values[1:], values[:1]], 0)
    shifted = pltpu.roll(values, extent - 1, axis)
    if axis == 2:
        lane = lax.broadcasted_iota(jnp.int32, values.shape, 2)
        shifted = jnp.where(lane == extent - 1, 0.0, shifted)
    return shifted


def behind(values, axis):
    extent = values.shape[axis]
    if axis == 0:
        return jnp.concatenate([values[extent - 1 :], values[: extent - 1]], 0)
    shifted = pltpu.roll(values, 1, axis)
    if axis == 2:
        lane = lax.broadcasted_iota(jnp.int32, values.shape, 2)
        shifted = jnp.where(lane == 0, 0.0, shifted)
    return shifted


def leapfrog_kernel(
    dims, offsets, e_ref, h_ref, perm_ref, cond_ref, xlo_ref, xhi_ref, ylo_ref, yhi_ref,
    cell_ref, fwd_ref, e_out, h_out, prod_out, ring,
):
    depth_x, depth_y, n_x, n_y = dims
    ring_x, ring_y = ring.shape[1], ring.shape[2]
    ring[0:3, 0:depth_x, 0:depth_y] = e_ref[...]
    ring[3:6, 0:depth_x, 0:depth_y] = h_ref[...]
    ring[6:9, 0:depth_x, 0:depth_y] = perm_ref[...]
    ring[9:10, 0:depth_x, 0:depth_y] = cond_ref[...]
    ring[:, depth_x : depth_x + HALO, 0:depth_y] = xhi_ref[...]
    ring[:, ring_x - HALO : ring_x, 0:depth_y] = xlo_ref[...]
    ring[:, :, depth_y : depth_y + HALO] = yhi_ref[...]
    ring[:, :, depth_y + HALO : ring_y - HALO] = jnp.zeros(
        (ring.shape[0], ring_x, ring_y - depth_y - 2 * HALO, LANES), jnp.float32
    )
    ring[:, :, ring_y - HALO : ring_y] = ylo_ref[...]

    shape = (ring_x, ring_y, LANES)
    xi = lax.broadcasted_iota(jnp.int32, shape, 0)
    yi = lax.broadcasted_iota(jnp.int32, shape, 1)
    gx = offsets[0] + jnp.where(xi < depth_x + HALO, xi, xi - ring_x)
    gy = offsets[1] + jnp.where(yi < depth_y + HALO, yi, yi - ring_y)
    y_real = (yi < depth_y + HALO) | (yi >= ring_y - HALO)
    inside = (gx >= 0) & (gx < n_x) & (gy >= 0) & (gy < n_y) & y_real

    field_e = [ring[c] for c in range(3)]
    field_h = [ring[3 + c] for c in range(3)]
    conductivity = ring[9]
    keep_rate, curl_gain = [], []
    for c in range(3):
        permittivity = jnp.where(inside, ring[6 + c], 1.0)
        ratio = 0.5 * conductivity / permittivity
        keep_rate.append((1.0 - ratio) / (1.0 + ratio))
        curl_gain.append(CE_GAIN / (permittivity * (1.0 + ratio)))

    cells = cell_ref[...]
    rows = depth_x * depth_y
    lane_pick = (lax.broadcasted_iota(jnp.int32, (LANES, cells.shape[1]), 0) == (cells % LANES)).astype(jnp.float32)
    row_pick = lax.broadcasted_iota(jnp.int32, (rows, cells.shape[1]), 0) == (cells // LANES)

    for step_index in range(STEPS):
        e0, e1, e2 = field_e
        curl = (
            (ahead(e2, 1) - e2) - (ahead(e1, 2) - e1),
            (ahead(e0, 2) - e0) - (ahead(e2, 0) - e2),
            (ahead(e1, 0) - e1) - (ahead(e0, 1) - e0),
        )
        field_h = [jnp.where(inside, field_h[c] - CH_GAIN * curl[c], 0.0) for c in range(3)]
        h0, h1, h2 = field_h
        curl = (
            (h2 - behind(h2, 1)) - (h1 - behind(h1, 2)),
            (h0 - behind(h0, 2)) - (h2 - behind(h2, 0)),
            (h1 - behind(h1, 0)) - (h0 - behind(h0, 1)),
        )
        field_e = [
            jnp.where(inside, keep_rate[c] * field_e[c] + curl_gain[c] * curl[c], 0.0) for c in range(3)
        ]
        product = None
        for c in range(3):
            block = field_e[c][0:depth_x, 0:depth_y].reshape(rows, LANES)
            by_lane = jnp.dot(block, lane_pick, precision=lax.Precision.HIGHEST, preferred_element_type=jnp.float32)
            picked = jnp.sum(jnp.where(row_pick, by_lane, 0.0), axis=0, keepdims=True)
            term = picked * fwd_ref[step_index, c : c + 1, :]
            product = term if product is None else product + term
        prod_out[step_index : step_index + 1, :] = product

    for c in range(3):
        e_out[c] = field_e[c][0:depth_x, 0:depth_y]
        h_out[c] = field_h[c][0:depth_x, 0:depth_y]


def leapfrog(offsets, field_e, field_h, permittivity, conductivity, xlo, xhi, ylo, yhi, cells, fwd, n_x, n_y):
    _, depth_x, depth_y, _ = field_e.shape
    ring_x = depth_x + 2 * HALO
    ring_y = -(-(depth_y + 2 * HALO) // 8) * 8
    vmem = pl.BlockSpec(memory_space=pltpu.VMEM)
    smem = pl.BlockSpec(memory_space=pltpu.SMEM)
    kernel = functools.partial(leapfrog_kernel, (depth_x, depth_y, n_x, n_y))
    return pl.pallas_call(
        kernel,
        out_shape=(
            jax.ShapeDtypeStruct(field_e.shape, jnp.float32),
            jax.ShapeDtypeStruct(field_h.shape, jnp.float32),
            jax.ShapeDtypeStruct((STEPS, cells.shape[1]), jnp.float32),
        ),
        in_specs=[smem] + [vmem] * 10,
        out_specs=(vmem, vmem, vmem),
        scratch_shapes=[pltpu.VMEM((10, ring_x, ring_y, LANES), jnp.float32)],
    )(offsets, field_e, field_h, permittivity, conductivity, xlo, xhi, ylo, yhi, cells, fwd)


def xor_rows(array, me, count, axis):
    bit = 1
    while bit < count:
        shape = array.shape[:axis] + (count // (2 * bit), 2, bit) + array.shape[axis + 1 :]
        split = array.reshape(shape)
        swapped = jnp.flip(split, axis + 1).reshape(array.shape)
        array = jnp.where((me // bit) % 2 == 1, swapped, array)
        bit *= 2
    return array


def exchange_by_halving(products, segments, count):
    me = lax.axis_index("slab")
    held = xor_rows(products, me, count, 1)[:, :, None]
    bit = count // 2
    while bit >= 1:
        owners = held.shape[1]
        keep = held[:, : owners // 2]
        send = held[:, owners // 2 :]
        pairs = [(i, i ^ bit) for i in range(count)]
        got = lax.ppermute(send, "slab", pairs)
        held = jnp.stack([keep, got], 3).reshape(keep.shape[:2] + (keep.shape[2] * 2,) + keep.shape[3:])
        bit //= 2
    return held[:, 0], xor_rows(segments, me, count, 0)


def shards(field_e, field_h, permittivity, conductivity, forward_e, slot_cell, recv_param):
    depth_x = field_e.shape[1]
    depth_y = field_e.shape[2]
    sources = recv_param.shape[2]
    capacity = recv_param.shape[3]
    n_x = lax.axis_size("slab") * depth_x
    n_y = lax.axis_size("yz") * depth_y
    parts = (field_e, field_h, permittivity, conductivity[None])
    xlo = recv_from(jnp.concatenate([p[:, depth_x - HALO :] for p in parts], 0), "slab", -1)
    xhi = recv_from(jnp.concatenate([p[:, :HALO] for p in parts], 0), "slab", 1)
    def rows(start):
        center = jnp.concatenate([p[:, :, start : start + HALO] for p in parts], 0)
        return jnp.concatenate([center, xhi[:, :, start : start + HALO], xlo[:, :, start : start + HALO]], 1)

    ylo = recv_from(rows(depth_y - HALO), "yz", -1)
    yhi = recv_from(rows(0), "yz", 1)
    offsets = jnp.stack([lax.axis_index("slab") * depth_x, lax.axis_index("yz") * depth_y]).astype(jnp.int32)
    new_e, new_h, products = leapfrog(
        offsets, field_e, field_h, permittivity, conductivity[None], xlo, xhi, ylo, yhi,
        slot_cell.reshape(1, -1), forward_e[0, 0], n_x, n_y,
    )
    products = products.reshape(STEPS, sources, capacity)
    segments = recv_param.reshape(sources, capacity)
    if sources & (sources - 1) == 0:
        received, segments = exchange_by_halving(products, segments, sources)
    else:
        received = lax.all_to_all(products, "slab", split_axis=1, concat_axis=1, tiled=True)
    segments = jnp.broadcast_to(segments[None], received.shape).reshape(-1, 1)
    params = lax.broadcasted_iota(jnp.int32, (1, PAR_DEV), 1)
    gradient = jnp.sum(jnp.where(segments == params, received.reshape(-1, 1), 0.0), axis=0)
    return (new_e, new_h, gradient.reshape(1, 1, PAR_DEV))


def solution(mesh):
    return jax.shard_map(
        shards,
        mesh=mesh,
        in_specs=(
            P(None, "slab", "yz", None),
            P(None, "slab", "yz", None),
            P(None, "slab", "yz", None),
            P("slab", "yz", None),
            P("slab", "yz", None, None, None),
            P("slab", "yz", None, None),
            P("slab", "yz", None, None),
        ),
        out_specs=(P(None, "slab", "yz", None), P(None, "slab", "yz", None), P("slab", "yz", None)),
        check_vma=False,
    )
```

```python
import functools

import jax
import jax.numpy as jnp
from jax import lax
from jax.experimental import pallas as pl
from jax.experimental.pallas import tpu as pltpu
from jax.sharding import PartitionSpec as P

STEPS = 2
PAR_DEV = 128
HALO = 2
LANES = 128
RADIX = 4

CH_GAIN = 0.5
CE_GAIN = 0.5


def recv_from(array, axis, offset):
    count = lax.axis_size(axis)
    pairs = [(i + offset, i) for i in range(count) if 0 <= i + offset < count]
    return lax.ppermute(array, axis, pairs)


def ahead(values, axis):
    extent = values.shape[axis]
    if axis == 0:
        return jnp.concatenate([values[1:], values[:1]], 0)
    shifted = pltpu.roll(values, extent - 1, axis)
    if axis == 2:
        lane = lax.broadcasted_iota(jnp.int32, values.shape, 2)
        shifted = jnp.where(lane == extent - 1, 0.0, shifted)
    return shifted


def behind(values, axis):
    extent = values.shape[axis]
    if axis == 0:
        return jnp.concatenate([values[extent - 1 :], values[: extent - 1]], 0)
    shifted = pltpu.roll(values, 1, axis)
    if axis == 2:
        lane = lax.broadcasted_iota(jnp.int32, values.shape, 2)
        shifted = jnp.where(lane == 0, 0.0, shifted)
    return shifted


def leapfrog_kernel(
    dims, offsets, e_ref, h_ref, perm_ref, cond_ref, xlo_ref, xhi_ref, ylo_ref, yhi_ref,
    cell_ref, fwd_ref, e_out, h_out, prod_out, ring,
):
    depth_x, depth_y, n_x, n_y = dims
    ring_x, ring_y = ring.shape[1], ring.shape[2]
    ring[0:3, 0:depth_x, 0:depth_y] = e_ref[...]
    ring[3:6, 0:depth_x, 0:depth_y] = h_ref[...]
    ring[6:9, 0:depth_x, 0:depth_y] = perm_ref[...]
    ring[9:10, 0:depth_x, 0:depth_y] = cond_ref[...]
    ring[:, depth_x : depth_x + HALO, 0:depth_y] = xhi_ref[...]
    ring[:, ring_x - HALO : ring_x, 0:depth_y] = xlo_ref[...]
    ring[:, :, depth_y : depth_y + HALO] = yhi_ref[...]
    ring[:, :, depth_y + HALO : ring_y - HALO] = jnp.zeros(
        (ring.shape[0], ring_x, ring_y - depth_y - 2 * HALO, LANES), jnp.float32
    )
    ring[:, :, ring_y - HALO : ring_y] = ylo_ref[...]

    shape = (ring_x, ring_y, LANES)
    xi = lax.broadcasted_iota(jnp.int32, shape, 0)
    yi = lax.broadcasted_iota(jnp.int32, shape, 1)
    gx = offsets[0] + jnp.where(xi < depth_x + HALO, xi, xi - ring_x)
    gy = offsets[1] + jnp.where(yi < depth_y + HALO, yi, yi - ring_y)
    y_real = (yi < depth_y + HALO) | (yi >= ring_y - HALO)
    inside = (gx >= 0) & (gx < n_x) & (gy >= 0) & (gy < n_y) & y_real

    field_e = [ring[c] for c in range(3)]
    field_h = [ring[3 + c] for c in range(3)]
    conductivity = ring[9]
    keep_rate, curl_gain = [], []
    for c in range(3):
        permittivity = jnp.where(inside, ring[6 + c], 1.0)
        ratio = 0.5 * conductivity / permittivity
        keep_rate.append((1.0 - ratio) / (1.0 + ratio))
        curl_gain.append(CE_GAIN / (permittivity * (1.0 + ratio)))

    cells = cell_ref[...]
    rows = depth_x * depth_y
    lane_pick = (lax.broadcasted_iota(jnp.int32, (LANES, cells.shape[1]), 0) == (cells % LANES)).astype(jnp.float32)
    row_pick = lax.broadcasted_iota(jnp.int32, (rows, cells.shape[1]), 0) == (cells // LANES)

    for step_index in range(STEPS):
        e0, e1, e2 = field_e
        curl = (
            (ahead(e2, 1) - e2) - (ahead(e1, 2) - e1),
            (ahead(e0, 2) - e0) - (ahead(e2, 0) - e2),
            (ahead(e1, 0) - e1) - (ahead(e0, 1) - e0),
        )
        field_h = [jnp.where(inside, field_h[c] - CH_GAIN * curl[c], 0.0) for c in range(3)]
        h0, h1, h2 = field_h
        curl = (
            (h2 - behind(h2, 1)) - (h1 - behind(h1, 2)),
            (h0 - behind(h0, 2)) - (h2 - behind(h2, 0)),
            (h1 - behind(h1, 0)) - (h0 - behind(h0, 1)),
        )
        field_e = [
            jnp.where(inside, keep_rate[c] * field_e[c] + curl_gain[c] * curl[c], 0.0) for c in range(3)
        ]
        product = None
        for c in range(3):
            block = field_e[c][0:depth_x, 0:depth_y].reshape(rows, LANES)
            by_lane = jnp.dot(block, lane_pick, precision=lax.Precision.HIGHEST, preferred_element_type=jnp.float32)
            picked = jnp.sum(jnp.where(row_pick, by_lane, 0.0), axis=0, keepdims=True)
            term = picked * fwd_ref[step_index, c : c + 1, :]
            product = term if product is None else product + term
        prod_out[step_index : step_index + 1, :] = product

    for c in range(3):
        e_out[c] = field_e[c][0:depth_x, 0:depth_y]
        h_out[c] = field_h[c][0:depth_x, 0:depth_y]


def leapfrog(offsets, field_e, field_h, permittivity, conductivity, xlo, xhi, ylo, yhi, cells, fwd, n_x, n_y):
    _, depth_x, depth_y, _ = field_e.shape
    ring_x = depth_x + 2 * HALO
    ring_y = -(-(depth_y + 2 * HALO) // 8) * 8
    vmem = pl.BlockSpec(memory_space=pltpu.VMEM)
    smem = pl.BlockSpec(memory_space=pltpu.SMEM)
    kernel = functools.partial(leapfrog_kernel, (depth_x, depth_y, n_x, n_y))
    return pl.pallas_call(
        kernel,
        out_shape=(
            jax.ShapeDtypeStruct(field_e.shape, jnp.float32),
            jax.ShapeDtypeStruct(field_h.shape, jnp.float32),
            jax.ShapeDtypeStruct((STEPS, cells.shape[1]), jnp.float32),
        ),
        in_specs=[smem] + [vmem] * 10,
        out_specs=(vmem, vmem, vmem),
        scratch_shapes=[pltpu.VMEM((10, ring_x, ring_y, LANES), jnp.float32)],
    )(offsets, field_e, field_h, permittivity, conductivity, xlo, xhi, ylo, yhi, cells, fwd)


def xor_rows(array, me, count, axis):
    bit = 1
    while bit < count:
        shape = array.shape[:axis] + (count // (2 * bit), 2, bit) + array.shape[axis + 1 :]
        split = array.reshape(shape)
        swapped = jnp.flip(split, axis + 1).reshape(array.shape)
        array = jnp.where((me // bit) % 2 == 1, swapped, array)
        bit *= 2
    return array


def exchange_by_halving(products, segments, count):
    me = lax.axis_index("slab")
    held = xor_rows(products, me, count, 1)[:, :, None]
    bit = count // 2
    while bit >= RADIX:
        owners = held.shape[1]
        keep = held[:, : owners // 2]
        send = held[:, owners // 2 :]
        pairs = [(i, i ^ bit) for i in range(count)]
        got = lax.ppermute(send, "slab", pairs)
        held = jnp.stack([keep, got], 3).reshape(keep.shape[:2] + (keep.shape[2] * 2,) + keep.shape[3:])
        bit //= 2
    owners = held.shape[1]
    pieces = [held[:, 0]]
    for q in range(1, owners):
        pieces.append(lax.ppermute(held[:, q], "slab", [(i, i ^ q) for i in range(count)]))
    held = jnp.stack(pieces, 2)
    held = held.reshape(held.shape[:1] + (held.shape[1] * owners,) + held.shape[3:])
    return held, xor_rows(segments, me, count, 0)


def shards(field_e, field_h, permittivity, conductivity, forward_e, slot_cell, recv_param):
    depth_x = field_e.shape[1]
    depth_y = field_e.shape[2]
    sources = recv_param.shape[2]
    capacity = recv_param.shape[3]
    n_x = lax.axis_size("slab") * depth_x
    n_y = lax.axis_size("yz") * depth_y
    parts = (field_e, field_h, permittivity, conductivity[None])
    xlo = recv_from(jnp.concatenate([p[:, depth_x - HALO :] for p in parts], 0), "slab", -1)
    xhi = recv_from(jnp.concatenate([p[:, :HALO] for p in parts], 0), "slab", 1)
    def rows(start):
        center = jnp.concatenate([p[:, :, start : start + HALO] for p in parts], 0)
        return jnp.concatenate([center, xhi[:, :, start : start + HALO], xlo[:, :, start : start + HALO]], 1)

    ylo = recv_from(rows(depth_y - HALO), "yz", -1)
    yhi = recv_from(rows(0), "yz", 1)
    offsets = jnp.stack([lax.axis_index("slab") * depth_x, lax.axis_index("yz") * depth_y]).astype(jnp.int32)
    new_e, new_h, products = leapfrog(
        offsets, field_e, field_h, permittivity, conductivity[None], xlo, xhi, ylo, yhi,
        slot_cell.reshape(1, -1), forward_e[0, 0], n_x, n_y,
    )
    products = products.reshape(STEPS, sources, capacity)
    segments = recv_param.reshape(sources, capacity)
    if sources & (sources - 1) == 0:
        received, segments = exchange_by_halving(products, segments, sources)
    else:
        received = lax.all_to_all(products, "slab", split_axis=1, concat_axis=1, tiled=True)
    segments = jnp.broadcast_to(segments[None], received.shape).reshape(-1, 1)
    params = lax.broadcasted_iota(jnp.int32, (1, PAR_DEV), 1)
    gradient = jnp.sum(jnp.where(segments == params, received.reshape(-1, 1), 0.0), axis=0)
    return (new_e, new_h, gradient.reshape(1, 1, PAR_DEV))


def solution(mesh):
    return jax.shard_map(
        shards,
        mesh=mesh,
        in_specs=(
            P(None, "slab", "yz", None),
            P(None, "slab", "yz", None),
            P(None, "slab", "yz", None),
            P("slab", "yz", None),
            P("slab", "yz", None, None, None),
            P("slab", "yz", None, None),
            P("slab", "yz", None, None),
        ),
        out_specs=(P(None, "slab", "yz", None), P(None, "slab", "yz", None), P("slab", "yz", None)),
        check_vma=False,
    )
```

```python
import functools

import jax
import jax.numpy as jnp
from jax import lax
from jax.experimental import pallas as pl
from jax.experimental.pallas import tpu as pltpu
from jax.sharding import PartitionSpec as P

STEPS = 2
PAR_DEV = 128
HALO = 2
LANES = 128
RADIX = 8

CH_GAIN = 0.5
CE_GAIN = 0.5


def recv_from(array, axis, offset):
    count = lax.axis_size(axis)
    pairs = [(i + offset, i) for i in range(count) if 0 <= i + offset < count]
    return lax.ppermute(array, axis, pairs)


def ahead(values, axis):
    extent = values.shape[axis]
    if axis == 0:
        return jnp.concatenate([values[1:], values[:1]], 0)
    shifted = pltpu.roll(values, extent - 1, axis)
    if axis == 2:
        lane = lax.broadcasted_iota(jnp.int32, values.shape, 2)
        shifted = jnp.where(lane == extent - 1, 0.0, shifted)
    return shifted


def behind(values, axis):
    extent = values.shape[axis]
    if axis == 0:
        return jnp.concatenate([values[extent - 1 :], values[: extent - 1]], 0)
    shifted = pltpu.roll(values, 1, axis)
    if axis == 2:
        lane = lax.broadcasted_iota(jnp.int32, values.shape, 2)
        shifted = jnp.where(lane == 0, 0.0, shifted)
    return shifted


def leapfrog_kernel(
    dims, offsets, e_ref, h_ref, perm_ref, cond_ref, xlo_ref, xhi_ref, ylo_ref, yhi_ref,
    cell_ref, fwd_ref, e_out, h_out, prod_out, ring,
):
    depth_x, depth_y, n_x, n_y = dims
    ring_x, ring_y = ring.shape[1], ring.shape[2]
    ring[0:3, 0:depth_x, 0:depth_y] = e_ref[...]
    ring[3:6, 0:depth_x, 0:depth_y] = h_ref[...]
    ring[6:9, 0:depth_x, 0:depth_y] = perm_ref[...]
    ring[9:10, 0:depth_x, 0:depth_y] = cond_ref[...]
    ring[:, depth_x : depth_x + HALO, 0:depth_y] = xhi_ref[...]
    ring[:, ring_x - HALO : ring_x, 0:depth_y] = xlo_ref[...]
    ring[:, :, depth_y : depth_y + HALO] = yhi_ref[...]
    ring[:, :, depth_y + HALO : ring_y - HALO] = jnp.zeros(
        (ring.shape[0], ring_x, ring_y - depth_y - 2 * HALO, LANES), jnp.float32
    )
    ring[:, :, ring_y - HALO : ring_y] = ylo_ref[...]

    shape = (ring_x, ring_y, LANES)
    xi = lax.broadcasted_iota(jnp.int32, shape, 0)
    yi = lax.broadcasted_iota(jnp.int32, shape, 1)
    gx = offsets[0] + jnp.where(xi < depth_x + HALO, xi, xi - ring_x)
    gy = offsets[1] + jnp.where(yi < depth_y + HALO, yi, yi - ring_y)
    y_real = (yi < depth_y + HALO) | (yi >= ring_y - HALO)
    inside = (gx >= 0) & (gx < n_x) & (gy >= 0) & (gy < n_y) & y_real

    field_e = [ring[c] for c in range(3)]
    field_h = [ring[3 + c] for c in range(3)]
    conductivity = ring[9]
    keep_rate, curl_gain = [], []
    for c in range(3):
        permittivity = jnp.where(inside, ring[6 + c], 1.0)
        ratio = 0.5 * conductivity / permittivity
        keep_rate.append((1.0 - ratio) / (1.0 + ratio))
        curl_gain.append(CE_GAIN / (permittivity * (1.0 + ratio)))

    cells = cell_ref[...]
    rows = depth_x * depth_y
    lane_pick = (lax.broadcasted_iota(jnp.int32, (LANES, cells.shape[1]), 0) == (cells % LANES)).astype(jnp.float32)
    row_pick = lax.broadcasted_iota(jnp.int32, (rows, cells.shape[1]), 0) == (cells // LANES)

    for step_index in range(STEPS):
        e0, e1, e2 = field_e
        curl = (
            (ahead(e2, 1) - e2) - (ahead(e1, 2) - e1),
            (ahead(e0, 2) - e0) - (ahead(e2, 0) - e2),
            (ahead(e1, 0) - e1) - (ahead(e0, 1) - e0),
        )
        field_h = [jnp.where(inside, field_h[c] - CH_GAIN * curl[c], 0.0) for c in range(3)]
        h0, h1, h2 = field_h
        curl = (
            (h2 - behind(h2, 1)) - (h1 - behind(h1, 2)),
            (h0 - behind(h0, 2)) - (h2 - behind(h2, 0)),
            (h1 - behind(h1, 0)) - (h0 - behind(h0, 1)),
        )
        field_e = [
            jnp.where(inside, keep_rate[c] * field_e[c] + curl_gain[c] * curl[c], 0.0) for c in range(3)
        ]
        product = None
        for c in range(3):
            block = field_e[c][0:depth_x, 0:depth_y].reshape(rows, LANES)
            by_lane = jnp.dot(block, lane_pick, precision=lax.Precision.HIGHEST, preferred_element_type=jnp.float32)
            picked = jnp.sum(jnp.where(row_pick, by_lane, 0.0), axis=0, keepdims=True)
            term = picked * fwd_ref[step_index, c : c + 1, :]
            product = term if product is None else product + term
        prod_out[step_index : step_index + 1, :] = product

    for c in range(3):
        e_out[c] = field_e[c][0:depth_x, 0:depth_y]
        h_out[c] = field_h[c][0:depth_x, 0:depth_y]


def leapfrog(offsets, field_e, field_h, permittivity, conductivity, xlo, xhi, ylo, yhi, cells, fwd, n_x, n_y):
    _, depth_x, depth_y, _ = field_e.shape
    ring_x = depth_x + 2 * HALO
    ring_y = -(-(depth_y + 2 * HALO) // 8) * 8
    vmem = pl.BlockSpec(memory_space=pltpu.VMEM)
    smem = pl.BlockSpec(memory_space=pltpu.SMEM)
    kernel = functools.partial(leapfrog_kernel, (depth_x, depth_y, n_x, n_y))
    return pl.pallas_call(
        kernel,
        out_shape=(
            jax.ShapeDtypeStruct(field_e.shape, jnp.float32),
            jax.ShapeDtypeStruct(field_h.shape, jnp.float32),
            jax.ShapeDtypeStruct((STEPS, cells.shape[1]), jnp.float32),
        ),
        in_specs=[smem] + [vmem] * 10,
        out_specs=(vmem, vmem, vmem),
        scratch_shapes=[pltpu.VMEM((10, ring_x, ring_y, LANES), jnp.float32)],
    )(offsets, field_e, field_h, permittivity, conductivity, xlo, xhi, ylo, yhi, cells, fwd)


def xor_rows(array, me, count, axis):
    bit = 1
    while bit < count:
        shape = array.shape[:axis] + (count // (2 * bit), 2, bit) + array.shape[axis + 1 :]
        split = array.reshape(shape)
        swapped = jnp.flip(split, axis + 1).reshape(array.shape)
        array = jnp.where((me // bit) % 2 == 1, swapped, array)
        bit *= 2
    return array


def exchange_by_halving(products, segments, count):
    me = lax.axis_index("slab")
    held = xor_rows(products, me, count, 1)[:, :, None]
    bit = count // 2
    while bit >= RADIX:
        owners = held.shape[1]
        keep = held[:, : owners // 2]
        send = held[:, owners // 2 :]
        pairs = [(i, i ^ bit) for i in range(count)]
        got = lax.ppermute(send, "slab", pairs)
        held = jnp.stack([keep, got], 3).reshape(keep.shape[:2] + (keep.shape[2] * 2,) + keep.shape[3:])
        bit //= 2
    owners = held.shape[1]
    pieces = [held[:, 0]]
    for q in range(1, owners):
        pieces.append(lax.ppermute(held[:, q], "slab", [(i, i ^ q) for i in range(count)]))
    held = jnp.stack(pieces, 2)
    held = held.reshape(held.shape[:1] + (held.shape[1] * owners,) + held.shape[3:])
    return held, xor_rows(segments, me, count, 0)


def shards(field_e, field_h, permittivity, conductivity, forward_e, slot_cell, recv_param):
    depth_x = field_e.shape[1]
    depth_y = field_e.shape[2]
    sources = recv_param.shape[2]
    capacity = recv_param.shape[3]
    n_x = lax.axis_size("slab") * depth_x
    n_y = lax.axis_size("yz") * depth_y
    parts = (field_e, field_h, permittivity, conductivity[None])
    xlo = recv_from(jnp.concatenate([p[:, depth_x - HALO :] for p in parts], 0), "slab", -1)
    xhi = recv_from(jnp.concatenate([p[:, :HALO] for p in parts], 0), "slab", 1)
    def rows(start):
        center = jnp.concatenate([p[:, :, start : start + HALO] for p in parts], 0)
        return jnp.concatenate([center, xhi[:, :, start : start + HALO], xlo[:, :, start : start + HALO]], 1)

    ylo = recv_from(rows(depth_y - HALO), "yz", -1)
    yhi = recv_from(rows(0), "yz", 1)
    offsets = jnp.stack([lax.axis_index("slab") * depth_x, lax.axis_index("yz") * depth_y]).astype(jnp.int32)
    new_e, new_h, products = leapfrog(
        offsets, field_e, field_h, permittivity, conductivity[None], xlo, xhi, ylo, yhi,
        slot_cell.reshape(1, -1), forward_e[0, 0], n_x, n_y,
    )
    products = products.reshape(STEPS, sources, capacity)
    segments = recv_param.reshape(sources, capacity)
    if sources & (sources - 1) == 0:
        received, segments = exchange_by_halving(products, segments, sources)
    else:
        received = lax.all_to_all(products, "slab", split_axis=1, concat_axis=1, tiled=True)
    segments = jnp.broadcast_to(segments[None], received.shape).reshape(-1, 1)
    params = lax.broadcasted_iota(jnp.int32, (1, PAR_DEV), 1)
    gradient = jnp.sum(jnp.where(segments == params, received.reshape(-1, 1), 0.0), axis=0)
    return (new_e, new_h, gradient.reshape(1, 1, PAR_DEV))


def solution(mesh):
    return jax.shard_map(
        shards,
        mesh=mesh,
        in_specs=(
            P(None, "slab", "yz", None),
            P(None, "slab", "yz", None),
            P(None, "slab", "yz", None),
            P("slab", "yz", None),
            P("slab", "yz", None, None, None),
            P("slab", "yz", None, None),
            P("slab", "yz", None, None),
        ),
        out_specs=(P(None, "slab", "yz", None), P(None, "slab", "yz", None), P("slab", "yz", None)),
        check_vma=False,
    )
```

```python
import functools

import jax
import jax.numpy as jnp
from jax import lax
from jax.experimental import pallas as pl
from jax.experimental.pallas import tpu as pltpu
from jax.sharding import PartitionSpec as P

STEPS = 2
PAR_DEV = 128
HALO = 2
LANES = 128
RADIX = 4

CH_GAIN = 0.5
CE_GAIN = 0.5


def recv_from(array, axis, offset):
    count = lax.axis_size(axis)
    pairs = [(i + offset, i) for i in range(count) if 0 <= i + offset < count]
    return lax.ppermute(array, axis, pairs)


def ahead(values, axis):
    extent = values.shape[axis]
    if axis == 0:
        return jnp.concatenate([values[1:], values[:1]], 0)
    shifted = pltpu.roll(values, extent - 1, axis)
    if axis == 2:
        lane = lax.broadcasted_iota(jnp.int32, values.shape, 2)
        shifted = jnp.where(lane == extent - 1, 0.0, shifted)
    return shifted


def behind(values, axis):
    extent = values.shape[axis]
    if axis == 0:
        return jnp.concatenate([values[extent - 1 :], values[: extent - 1]], 0)
    shifted = pltpu.roll(values, 1, axis)
    if axis == 2:
        lane = lax.broadcasted_iota(jnp.int32, values.shape, 2)
        shifted = jnp.where(lane == 0, 0.0, shifted)
    return shifted


def swap_halos(first, last, axis):
    count = lax.axis_size(axis)
    odd = lax.axis_index(axis) % 2 == 1
    inner = [(i, i ^ 1) for i in range(count) if i ^ 1 < count]
    outer = [p for i in range(1, count - 1, 2) for p in ((i, i + 1), (i + 1, i))]
    got_inner = lax.ppermute(jnp.where(odd, first, last), axis, inner)
    got_outer = lax.ppermute(jnp.where(odd, last, first), axis, outer)
    low = jnp.where(odd, got_inner, got_outer)
    high = jnp.where(odd, got_outer, got_inner)
    return low, high


def leapfrog_kernel(
    dims, offsets, e_ref, h_ref, perm_ref, cond_ref, xlo_ref, xhi_ref, ylo_ref, yhi_ref,
    cell_ref, fwd_ref, e_out, h_out, prod_out, ring,
):
    depth_x, depth_y, n_x, n_y = dims
    ring_x, ring_y = ring.shape[1], ring.shape[2]
    ring[0:3, 0:depth_x, 0:depth_y] = e_ref[...]
    ring[3:6, 0:depth_x, 0:depth_y] = h_ref[...]
    ring[6:9, 0:depth_x, 0:depth_y] = perm_ref[...]
    ring[9:10, 0:depth_x, 0:depth_y] = cond_ref[...]
    ring[:, depth_x : depth_x + HALO, 0:depth_y] = xhi_ref[...]
    ring[:, ring_x - HALO : ring_x, 0:depth_y] = xlo_ref[...]
    ring[:, :, depth_y : depth_y + HALO] = yhi_ref[...]
    ring[:, :, depth_y + HALO : ring_y - HALO] = jnp.zeros(
        (ring.shape[0], ring_x, ring_y - depth_y - 2 * HALO, LANES), jnp.float32
    )
    ring[:, :, ring_y - HALO : ring_y] = ylo_ref[...]

    shape = (ring_x, ring_y, LANES)
    xi = lax.broadcasted_iota(jnp.int32, shape, 0)
    yi = lax.broadcasted_iota(jnp.int32, shape, 1)
    gx = offsets[0] + jnp.where(xi < depth_x + HALO, xi, xi - ring_x)
    gy = offsets[1] + jnp.where(yi < depth_y + HALO, yi, yi - ring_y)
    y_real = (yi < depth_y + HALO) | (yi >= ring_y - HALO)
    inside = (gx >= 0) & (gx < n_x) & (gy >= 0) & (gy < n_y) & y_real

    field_e = [ring[c] for c in range(3)]
    field_h = [ring[3 + c] for c in range(3)]
    conductivity = ring[9]
    keep_rate, curl_gain = [], []
    for c in range(3):
        permittivity = jnp.where(inside, ring[6 + c], 1.0)
        ratio = 0.5 * conductivity / permittivity
        keep_rate.append((1.0 - ratio) / (1.0 + ratio))
        curl_gain.append(CE_GAIN / (permittivity * (1.0 + ratio)))

    cells = cell_ref[...]
    rows = depth_x * depth_y
    lane_pick = (lax.broadcasted_iota(jnp.int32, (LANES, cells.shape[1]), 0) == (cells % LANES)).astype(jnp.float32)
    row_pick = lax.broadcasted_iota(jnp.int32, (rows, cells.shape[1]), 0) == (cells // LANES)

    for step_index in range(STEPS):
        e0, e1, e2 = field_e
        curl = (
            (ahead(e2, 1) - e2) - (ahead(e1, 2) - e1),
            (ahead(e0, 2) - e0) - (ahead(e2, 0) - e2),
            (ahead(e1, 0) - e1) - (ahead(e0, 1) - e0),
        )
        field_h = [jnp.where(inside, field_h[c] - CH_GAIN * curl[c], 0.0) for c in range(3)]
        h0, h1, h2 = field_h
        curl = (
            (h2 - behind(h2, 1)) - (h1 - behind(h1, 2)),
            (h0 - behind(h0, 2)) - (h2 - behind(h2, 0)),
            (h1 - behind(h1, 0)) - (h0 - behind(h0, 1)),
        )
        field_e = [
            jnp.where(inside, keep_rate[c] * field_e[c] + curl_gain[c] * curl[c], 0.0) for c in range(3)
        ]
        product = None
        for c in range(3):
            block = field_e[c][0:depth_x, 0:depth_y].reshape(rows, LANES)
            by_lane = jnp.dot(block, lane_pick, precision=lax.Precision.HIGHEST, preferred_element_type=jnp.float32)
            picked = jnp.sum(jnp.where(row_pick, by_lane, 0.0), axis=0, keepdims=True)
            term = picked * fwd_ref[step_index, c : c + 1, :]
            product = term if product is None else product + term
        prod_out[step_index : step_index + 1, :] = product

    for c in range(3):
        e_out[c] = field_e[c][0:depth_x, 0:depth_y]
        h_out[c] = field_h[c][0:depth_x, 0:depth_y]


def leapfrog(offsets, field_e, field_h, permittivity, conductivity, xlo, xhi, ylo, yhi, cells, fwd, n_x, n_y):
    _, depth_x, depth_y, _ = field_e.shape
    ring_x = depth_x + 2 * HALO
    ring_y = -(-(depth_y + 2 * HALO) // 8) * 8
    vmem = pl.BlockSpec(memory_space=pltpu.VMEM)
    smem = pl.BlockSpec(memory_space=pltpu.SMEM)
    kernel = functools.partial(leapfrog_kernel, (depth_x, depth_y, n_x, n_y))
    return pl.pallas_call(
        kernel,
        out_shape=(
            jax.ShapeDtypeStruct(field_e.shape, jnp.float32),
            jax.ShapeDtypeStruct(field_h.shape, jnp.float32),
            jax.ShapeDtypeStruct((STEPS, cells.shape[1]), jnp.float32),
        ),
        in_specs=[smem] + [vmem] * 10,
        out_specs=(vmem, vmem, vmem),
        scratch_shapes=[pltpu.VMEM((10, ring_x, ring_y, LANES), jnp.float32)],
    )(offsets, field_e, field_h, permittivity, conductivity, xlo, xhi, ylo, yhi, cells, fwd)


def xor_rows(array, me, count, axis):
    bit = 1
    while bit < count:
        shape = array.shape[:axis] + (count // (2 * bit), 2, bit) + array.shape[axis + 1 :]
        split = array.reshape(shape)
        swapped = jnp.flip(split, axis + 1).reshape(array.shape)
        array = jnp.where((me // bit) % 2 == 1, swapped, array)
        bit *= 2
    return array


def exchange_by_halving(products, segments, count):
    me = lax.axis_index("slab")
    held = xor_rows(products, me, count, 1)[:, :, None]
    bit = count // 2
    while bit >= RADIX:
        owners = held.shape[1]
        keep = held[:, : owners // 2]
        send = held[:, owners // 2 :]
        pairs = [(i, i ^ bit) for i in range(count)]
        got = lax.ppermute(send, "slab", pairs)
        held = jnp.stack([keep, got], 3).reshape(keep.shape[:2] + (keep.shape[2] * 2,) + keep.shape[3:])
        bit //= 2
    owners = held.shape[1]
    pieces = [held[:, 0]]
    for q in range(1, owners):
        pieces.append(lax.ppermute(held[:, q], "slab", [(i, i ^ q) for i in range(count)]))
    held = jnp.stack(pieces, 2)
    held = held.reshape(held.shape[:1] + (held.shape[1] * owners,) + held.shape[3:])
    return held, xor_rows(segments, me, count, 0)


def shards(field_e, field_h, permittivity, conductivity, forward_e, slot_cell, recv_param):
    depth_x = field_e.shape[1]
    depth_y = field_e.shape[2]
    sources = recv_param.shape[2]
    capacity = recv_param.shape[3]
    n_x = lax.axis_size("slab") * depth_x
    n_y = lax.axis_size("yz") * depth_y
    parts = (field_e, field_h, permittivity, conductivity[None])
    xlo, xhi = swap_halos(
        jnp.concatenate([p[:, :HALO] for p in parts], 0),
        jnp.concatenate([p[:, depth_x - HALO :] for p in parts], 0),
        "slab",
    )
    def rows(start):
        center = jnp.concatenate([p[:, :, start : start + HALO] for p in parts], 0)
        return jnp.concatenate([center, xhi[:, :, start : start + HALO], xlo[:, :, start : start + HALO]], 1)

    ylo, yhi = swap_halos(rows(0), rows(depth_y - HALO), "yz")
    offsets = jnp.stack([lax.axis_index("slab") * depth_x, lax.axis_index("yz") * depth_y]).astype(jnp.int32)
    new_e, new_h, products = leapfrog(
        offsets, field_e, field_h, permittivity, conductivity[None], xlo, xhi, ylo, yhi,
        slot_cell.reshape(1, -1), forward_e[0, 0], n_x, n_y,
    )
    products = products.reshape(STEPS, sources, capacity)
    segments = recv_param.reshape(sources, capacity)
    if sources & (sources - 1) == 0:
        received, segments = exchange_by_halving(products, segments, sources)
    else:
        received = lax.all_to_all(products, "slab", split_axis=1, concat_axis=1, tiled=True)
    segments = jnp.broadcast_to(segments[None], received.shape).reshape(-1, 1)
    params = lax.broadcasted_iota(jnp.int32, (1, PAR_DEV), 1)
    gradient = jnp.sum(jnp.where(segments == params, received.reshape(-1, 1), 0.0), axis=0)
    return (new_e, new_h, gradient.reshape(1, 1, PAR_DEV))


def solution(mesh):
    return jax.shard_map(
        shards,
        mesh=mesh,
        in_specs=(
            P(None, "slab", "yz", None),
            P(None, "slab", "yz", None),
            P(None, "slab", "yz", None),
            P("slab", "yz", None),
            P("slab", "yz", None, None, None),
            P("slab", "yz", None, None),
            P("slab", "yz", None, None),
        ),
        out_specs=(P(None, "slab", "yz", None), P(None, "slab", "yz", None), P("slab", "yz", None)),
        check_vma=False,
    )
```

```python
import functools

import jax
import jax.numpy as jnp
from jax import lax
from jax.experimental import pallas as pl
from jax.experimental.pallas import tpu as pltpu
from jax.sharding import PartitionSpec as P

STEPS = 2
PAR_DEV = 128
HALO = 2
LANES = 128
RADIX = 4

CH_GAIN = 0.5
CE_GAIN = 0.5


def recv_from(array, axis, offset):
    count = lax.axis_size(axis)
    pairs = [(i + offset, i) for i in range(count) if 0 <= i + offset < count]
    return lax.ppermute(array, axis, pairs)


def ahead(values, axis):
    extent = values.shape[axis]
    if axis == 0:
        return jnp.concatenate([values[1:], values[:1]], 0)
    shifted = pltpu.roll(values, extent - 1, axis)
    if axis == 2:
        lane = lax.broadcasted_iota(jnp.int32, values.shape, 2)
        shifted = jnp.where(lane == extent - 1, 0.0, shifted)
    return shifted


def behind(values, axis):
    extent = values.shape[axis]
    if axis == 0:
        return jnp.concatenate([values[extent - 1 :], values[: extent - 1]], 0)
    shifted = pltpu.roll(values, 1, axis)
    if axis == 2:
        lane = lax.broadcasted_iota(jnp.int32, values.shape, 2)
        shifted = jnp.where(lane == 0, 0.0, shifted)
    return shifted


def swap_halos(first, last, axis):
    count = lax.axis_size(axis)
    odd = lax.axis_index(axis) % 2 == 1
    inner = [(i, i ^ 1) for i in range(count) if i ^ 1 < count]
    outer = [p for i in range(1, count - 1, 2) for p in ((i, i + 1), (i + 1, i))]
    got_inner = lax.ppermute(jnp.where(odd, first, last), axis, inner)
    got_outer = lax.ppermute(jnp.where(odd, last, first), axis, outer)
    return got_inner, got_outer


def low_high(got_inner, got_outer, odd):
    return jnp.where(odd, got_inner, got_outer), jnp.where(odd, got_outer, got_inner)


def leapfrog_kernel(
    dims, e_ref, h_ref, perm_ref, cond_ref, x_inner_ref, x_outer_ref, y_inner_ref, y_outer_ref,
    cell_ref, fwd_ref, e_out, h_out, prod_out, ring,
):
    depth_x, depth_y, n_x, n_y = dims
    ring_x, ring_y = ring.shape[1], ring.shape[2]
    slab, yz = lax.axis_index("slab"), lax.axis_index("yz")
    xlo, xhi = low_high(x_inner_ref[...], x_outer_ref[...], slab % 2 == 1)
    ylo, yhi = low_high(y_inner_ref[...], y_outer_ref[...], yz % 2 == 1)
    ring[0:3, 0:depth_x, 0:depth_y] = e_ref[...]
    ring[3:6, 0:depth_x, 0:depth_y] = h_ref[...]
    ring[6:9, 0:depth_x, 0:depth_y] = perm_ref[...]
    ring[9:10, 0:depth_x, 0:depth_y] = cond_ref[...]
    ring[:, depth_x : depth_x + HALO, 0:depth_y] = xhi
    ring[:, ring_x - HALO : ring_x, 0:depth_y] = xlo
    ring[:, :, depth_y : depth_y + HALO] = yhi
    ring[:, :, depth_y + HALO : ring_y - HALO] = jnp.zeros(
        (ring.shape[0], ring_x, ring_y - depth_y - 2 * HALO, LANES), jnp.float32
    )
    ring[:, :, ring_y - HALO : ring_y] = ylo

    shape = (ring_x, ring_y, LANES)
    xi = lax.broadcasted_iota(jnp.int32, shape, 0)
    yi = lax.broadcasted_iota(jnp.int32, shape, 1)
    gx = slab * depth_x + jnp.where(xi < depth_x + HALO, xi, xi - ring_x)
    gy = yz * depth_y + jnp.where(yi < depth_y + HALO, yi, yi - ring_y)
    y_real = (yi < depth_y + HALO) | (yi >= ring_y - HALO)
    inside = (gx >= 0) & (gx < n_x) & (gy >= 0) & (gy < n_y) & y_real

    field_e = [ring[c] for c in range(3)]
    field_h = [ring[3 + c] for c in range(3)]
    conductivity = ring[9]
    keep_rate, curl_gain = [], []
    for c in range(3):
        permittivity = jnp.where(inside, ring[6 + c], 1.0)
        ratio = 0.5 * conductivity / permittivity
        keep_rate.append((1.0 - ratio) / (1.0 + ratio))
        curl_gain.append(CE_GAIN / (permittivity * (1.0 + ratio)))

    cells = cell_ref[...]
    rows = depth_x * depth_y
    lane_pick = (lax.broadcasted_iota(jnp.int32, (LANES, cells.shape[1]), 0) == (cells % LANES)).astype(jnp.float32)
    row_pick = lax.broadcasted_iota(jnp.int32, (rows, cells.shape[1]), 0) == (cells // LANES)

    for step_index in range(STEPS):
        e0, e1, e2 = field_e
        curl = (
            (ahead(e2, 1) - e2) - (ahead(e1, 2) - e1),
            (ahead(e0, 2) - e0) - (ahead(e2, 0) - e2),
            (ahead(e1, 0) - e1) - (ahead(e0, 1) - e0),
        )
        field_h = [jnp.where(inside, field_h[c] - CH_GAIN * curl[c], 0.0) for c in range(3)]
        h0, h1, h2 = field_h
        curl = (
            (h2 - behind(h2, 1)) - (h1 - behind(h1, 2)),
            (h0 - behind(h0, 2)) - (h2 - behind(h2, 0)),
            (h1 - behind(h1, 0)) - (h0 - behind(h0, 1)),
        )
        field_e = [
            jnp.where(inside, keep_rate[c] * field_e[c] + curl_gain[c] * curl[c], 0.0) for c in range(3)
        ]
        product = None
        for c in range(3):
            block = field_e[c][0:depth_x, 0:depth_y].reshape(rows, LANES)
            by_lane = jnp.dot(block, lane_pick, precision=lax.Precision.HIGHEST, preferred_element_type=jnp.float32)
            picked = jnp.sum(jnp.where(row_pick, by_lane, 0.0), axis=0, keepdims=True)
            term = picked * fwd_ref[step_index, c : c + 1, :]
            product = term if product is None else product + term
        prod_out[step_index : step_index + 1, :] = product

    for c in range(3):
        e_out[c] = field_e[c][0:depth_x, 0:depth_y]
        h_out[c] = field_h[c][0:depth_x, 0:depth_y]


def leapfrog(field_e, field_h, permittivity, conductivity, xlo, xhi, ylo, yhi, cells, fwd, n_x, n_y):
    _, depth_x, depth_y, _ = field_e.shape
    ring_x = depth_x + 2 * HALO
    ring_y = -(-(depth_y + 2 * HALO) // 8) * 8
    vmem = pl.BlockSpec(memory_space=pltpu.VMEM)
    kernel = functools.partial(leapfrog_kernel, (depth_x, depth_y, n_x, n_y))
    return pl.pallas_call(
        kernel,
        out_shape=(
            jax.ShapeDtypeStruct(field_e.shape, jnp.float32),
            jax.ShapeDtypeStruct(field_h.shape, jnp.float32),
            jax.ShapeDtypeStruct((STEPS, cells.shape[1]), jnp.float32),
        ),
        in_specs=[vmem] * 10,
        out_specs=(vmem, vmem, vmem),
        scratch_shapes=[pltpu.VMEM((10, ring_x, ring_y, LANES), jnp.float32)],
    )(field_e, field_h, permittivity, conductivity, xlo, xhi, ylo, yhi, cells, fwd)


def xor_rows(array, me, count, axis):
    bit = 1
    while bit < count:
        shape = array.shape[:axis] + (count // (2 * bit), 2, bit) + array.shape[axis + 1 :]
        split = array.reshape(shape)
        swapped = jnp.flip(split, axis + 1).reshape(array.shape)
        array = jnp.where((me // bit) % 2 == 1, swapped, array)
        bit *= 2
    return array


def exchange_by_halving(products, segments, count):
    me = lax.axis_index("slab")
    held = xor_rows(products, me, count, 1)[:, :, None]
    bit = count // 2
    while bit >= RADIX:
        owners = held.shape[1]
        keep = held[:, : owners // 2]
        send = held[:, owners // 2 :]
        pairs = [(i, i ^ bit) for i in range(count)]
        got = lax.ppermute(send, "slab", pairs)
        held = jnp.stack([keep, got], 3).reshape(keep.shape[:2] + (keep.shape[2] * 2,) + keep.shape[3:])
        bit //= 2
    owners = held.shape[1]
    pieces = [held[:, 0]]
    for q in range(1, owners):
        pieces.append(lax.ppermute(held[:, q], "slab", [(i, i ^ q) for i in range(count)]))
    held = jnp.stack(pieces, 2)
    held = held.reshape(held.shape[:1] + (held.shape[1] * owners,) + held.shape[3:])
    return held, xor_rows(segments, me, count, 0)


def shards(field_e, field_h, permittivity, conductivity, forward_e, slot_cell, recv_param):
    depth_x = field_e.shape[1]
    depth_y = field_e.shape[2]
    sources = recv_param.shape[2]
    capacity = recv_param.shape[3]
    n_x = lax.axis_size("slab") * depth_x
    n_y = lax.axis_size("yz") * depth_y
    parts = (field_e, field_h, permittivity, conductivity[None])
    x_inner, x_outer = swap_halos(
        jnp.concatenate([p[:, :HALO] for p in parts], 0),
        jnp.concatenate([p[:, depth_x - HALO :] for p in parts], 0),
        "slab",
    )
    xlo, xhi = low_high(x_inner, x_outer, lax.axis_index("slab") % 2 == 1)
    def rows(start):
        center = jnp.concatenate([p[:, :, start : start + HALO] for p in parts], 0)
        return jnp.concatenate([center, xhi[:, :, start : start + HALO], xlo[:, :, start : start + HALO]], 1)

    y_inner, y_outer = swap_halos(rows(0), rows(depth_y - HALO), "yz")
    new_e, new_h, products = leapfrog(
        field_e, field_h, permittivity, conductivity[None], x_inner, x_outer, y_inner, y_outer,
        slot_cell.reshape(1, -1), forward_e[0, 0], n_x, n_y,
    )
    products = products.reshape(STEPS, sources, capacity)
    segments = recv_param.reshape(sources, capacity)
    if sources & (sources - 1) == 0:
        received, segments = exchange_by_halving(products, segments, sources)
    else:
        received = lax.all_to_all(products, "slab", split_axis=1, concat_axis=1, tiled=True)
    segments = jnp.broadcast_to(segments[None], received.shape).reshape(-1, 1)
    params = lax.broadcasted_iota(jnp.int32, (1, PAR_DEV), 1)
    gradient = jnp.sum(jnp.where(segments == params, received.reshape(-1, 1), 0.0), axis=0)
    return (new_e, new_h, gradient.reshape(1, 1, PAR_DEV))


def solution(mesh):
    return jax.shard_map(
        shards,
        mesh=mesh,
        in_specs=(
            P(None, "slab", "yz", None),
            P(None, "slab", "yz", None),
            P(None, "slab", "yz", None),
            P("slab", "yz", None),
            P("slab", "yz", None, None, None),
            P("slab", "yz", None, None),
            P("slab", "yz", None, None),
        ),
        out_specs=(P(None, "slab", "yz", None), P(None, "slab", "yz", None), P("slab", "yz", None)),
        check_vma=False,
    )
```

```python
import functools

import jax
import jax.numpy as jnp
from jax import lax
from jax.experimental import pallas as pl
from jax.experimental.pallas import tpu as pltpu
from jax.sharding import PartitionSpec as P

STEPS = 2
PAR_DEV = 128
HALO = 2
LANES = 128
RADIX = 4

CH_GAIN = 0.5
CE_GAIN = 0.5


def recv_from(array, axis, offset):
    count = lax.axis_size(axis)
    pairs = [(i + offset, i) for i in range(count) if 0 <= i + offset < count]
    return lax.ppermute(array, axis, pairs)


def ahead(values, axis):
    extent = values.shape[axis]
    if axis == 0:
        return jnp.concatenate([values[1:], values[:1]], 0)
    shifted = pltpu.roll(values, extent - 1, axis)
    if axis == 2:
        lane = lax.broadcasted_iota(jnp.int32, values.shape, 2)
        shifted = jnp.where(lane == extent - 1, 0.0, shifted)
    return shifted


def behind(values, axis):
    extent = values.shape[axis]
    if axis == 0:
        return jnp.concatenate([values[extent - 1 :], values[: extent - 1]], 0)
    shifted = pltpu.roll(values, 1, axis)
    if axis == 2:
        lane = lax.broadcasted_iota(jnp.int32, values.shape, 2)
        shifted = jnp.where(lane == 0, 0.0, shifted)
    return shifted


def swap_halos(first, last, axis):
    count = lax.axis_size(axis)
    odd = lax.axis_index(axis) % 2 == 1
    inner = [(i, i ^ 1) for i in range(count) if i ^ 1 < count]
    outer = [p for i in range(1, count - 1, 2) for p in ((i, i + 1), (i + 1, i))]
    got_inner = lax.ppermute(jnp.where(odd, first, last), axis, inner)
    got_outer = lax.ppermute(jnp.where(odd, last, first), axis, outer)
    return got_inner, got_outer


def low_high(got_inner, got_outer, odd):
    return jnp.where(odd, got_inner, got_outer), jnp.where(odd, got_outer, got_inner)


def leapfrog_kernel(
    dims, e_ref, h_ref, perm_ref, cond_ref, x_inner_ref, x_outer_ref, y_inner_ref, y_outer_ref,
    cell_ref, fwd_ref, e_out, h_out, prod_out, ring,
):
    depth_x, depth_y, n_x, n_y = dims
    ring_x, ring_y = ring.shape[1], ring.shape[2]
    slab, yz = lax.axis_index("slab"), lax.axis_index("yz")
    xlo, xhi = low_high(x_inner_ref[...], x_outer_ref[...], slab % 2 == 1)
    ylo, yhi = low_high(y_inner_ref[...], y_outer_ref[...], yz % 2 == 1)
    ring[0:3, 0:depth_x, 0:depth_y] = e_ref[...]
    ring[3:6, 0:depth_x, 0:depth_y] = h_ref[...]
    ring[6:9, 0:depth_x, 0:depth_y] = perm_ref[...]
    ring[9:10, 0:depth_x, 0:depth_y] = cond_ref[...]
    ring[:, depth_x : depth_x + HALO, 0:depth_y] = xhi
    ring[:, ring_x - HALO : ring_x, 0:depth_y] = xlo
    ring[:, :, depth_y : depth_y + HALO] = yhi
    ring[:, :, depth_y + HALO : ring_y - HALO] = jnp.zeros(
        (ring.shape[0], ring_x, ring_y - depth_y - 2 * HALO, LANES), jnp.float32
    )
    ring[:, :, ring_y - HALO : ring_y] = ylo

    shape = (ring_x, ring_y, LANES)
    xi = lax.broadcasted_iota(jnp.int32, shape, 0)
    yi = lax.broadcasted_iota(jnp.int32, shape, 1)
    gx = slab * depth_x + jnp.where(xi < depth_x + HALO, xi, xi - ring_x)
    gy = yz * depth_y + jnp.where(yi < depth_y + HALO, yi, yi - ring_y)
    y_real = (yi < depth_y + HALO) | (yi >= ring_y - HALO)
    inside = (gx >= 0) & (gx < n_x) & (gy >= 0) & (gy < n_y) & y_real

    field_e = [ring[c] for c in range(3)]
    field_h = [ring[3 + c] for c in range(3)]
    conductivity = ring[9]
    keep_rate, curl_gain = [], []
    for c in range(3):
        permittivity = jnp.where(inside, ring[6 + c], 1.0)
        ratio = 0.5 * conductivity / permittivity
        keep_rate.append((1.0 - ratio) / (1.0 + ratio))
        curl_gain.append(CE_GAIN / (permittivity * (1.0 + ratio)))

    grid = cell_ref[...].astype(jnp.float32)
    owners, capacity = grid.shape
    slots = owners * capacity
    slot = lax.broadcasted_iota(jnp.int32, (capacity, slots), 1)
    spread = (slot % capacity == lax.broadcasted_iota(jnp.int32, (capacity, slots), 0)).astype(jnp.float32)
    by_owner = jnp.dot(grid, spread, precision=lax.Precision.HIGHEST, preferred_element_type=jnp.float32)
    mine = lax.broadcasted_iota(jnp.int32, (owners, slots), 1) // capacity == lax.broadcasted_iota(
        jnp.int32, (owners, slots), 0
    )
    cells = jnp.sum(jnp.where(mine, by_owner, 0.0), axis=0, keepdims=True).astype(jnp.int32)
    rows = depth_x * depth_y
    lane_pick = (lax.broadcasted_iota(jnp.int32, (LANES, cells.shape[1]), 0) == (cells % LANES)).astype(jnp.float32)
    row_pick = lax.broadcasted_iota(jnp.int32, (rows, cells.shape[1]), 0) == (cells // LANES)

    for step_index in range(STEPS):
        e0, e1, e2 = field_e
        curl = (
            (ahead(e2, 1) - e2) - (ahead(e1, 2) - e1),
            (ahead(e0, 2) - e0) - (ahead(e2, 0) - e2),
            (ahead(e1, 0) - e1) - (ahead(e0, 1) - e0),
        )
        field_h = [jnp.where(inside, field_h[c] - CH_GAIN * curl[c], 0.0) for c in range(3)]
        h0, h1, h2 = field_h
        curl = (
            (h2 - behind(h2, 1)) - (h1 - behind(h1, 2)),
            (h0 - behind(h0, 2)) - (h2 - behind(h2, 0)),
            (h1 - behind(h1, 0)) - (h0 - behind(h0, 1)),
        )
        field_e = [
            jnp.where(inside, keep_rate[c] * field_e[c] + curl_gain[c] * curl[c], 0.0) for c in range(3)
        ]
        product = None
        for c in range(3):
            block = field_e[c][0:depth_x, 0:depth_y].reshape(rows, LANES)
            by_lane = jnp.dot(block, lane_pick, precision=lax.Precision.HIGHEST, preferred_element_type=jnp.float32)
            picked = jnp.sum(jnp.where(row_pick, by_lane, 0.0), axis=0, keepdims=True)
            term = picked * fwd_ref[c, step_index : step_index + 1, :]
            product = term if product is None else product + term
        prod_out[step_index : step_index + 1, :] = product

    for c in range(3):
        e_out[c] = field_e[c][0:depth_x, 0:depth_y]
        h_out[c] = field_h[c][0:depth_x, 0:depth_y]


def leapfrog(field_e, field_h, permittivity, conductivity, xlo, xhi, ylo, yhi, cells, fwd, n_x, n_y):
    _, depth_x, depth_y, _ = field_e.shape
    ring_x = depth_x + 2 * HALO
    ring_y = -(-(depth_y + 2 * HALO) // 8) * 8
    vmem = pl.BlockSpec(memory_space=pltpu.VMEM)
    kernel = functools.partial(leapfrog_kernel, (depth_x, depth_y, n_x, n_y))
    return pl.pallas_call(
        kernel,
        out_shape=(
            jax.ShapeDtypeStruct(field_e.shape, jnp.float32),
            jax.ShapeDtypeStruct(field_h.shape, jnp.float32),
            jax.ShapeDtypeStruct((STEPS, cells.size), jnp.float32),
        ),
        in_specs=[vmem] * 10,
        out_specs=(vmem, vmem, vmem),
        scratch_shapes=[pltpu.VMEM((10, ring_x, ring_y, LANES), jnp.float32)],
    )(field_e, field_h, permittivity, conductivity, xlo, xhi, ylo, yhi, cells, fwd)


def xor_rows(array, me, count, axis):
    bit = 1
    while bit < count:
        shape = array.shape[:axis] + (count // (2 * bit), 2, bit) + array.shape[axis + 1 :]
        split = array.reshape(shape)
        swapped = jnp.flip(split, axis + 1).reshape(array.shape)
        array = jnp.where((me // bit) % 2 == 1, swapped, array)
        bit *= 2
    return array


def exchange_by_halving(products, segments, count):
    me = lax.axis_index("slab")
    held = xor_rows(products, me, count, 1)[:, :, None]
    bit = count // 2
    while bit >= RADIX:
        owners = held.shape[1]
        keep = held[:, : owners // 2]
        send = held[:, owners // 2 :]
        pairs = [(i, i ^ bit) for i in range(count)]
        got = lax.ppermute(send, "slab", pairs)
        held = jnp.stack([keep, got], 3).reshape(keep.shape[:2] + (keep.shape[2] * 2,) + keep.shape[3:])
        bit //= 2
    owners = held.shape[1]
    pieces = [held[:, 0]]
    for q in range(1, owners):
        pieces.append(lax.ppermute(held[:, q], "slab", [(i, i ^ q) for i in range(count)]))
    held = jnp.stack(pieces, 2)
    held = held.reshape(held.shape[:1] + (held.shape[1] * owners,) + held.shape[3:])
    return held, xor_rows(segments, me, count, 0)


def shards(field_e, field_h, permittivity, conductivity, forward_e, slot_cell, recv_param):
    depth_x = field_e.shape[1]
    depth_y = field_e.shape[2]
    sources = recv_param.shape[2]
    capacity = recv_param.shape[3]
    n_x = lax.axis_size("slab") * depth_x
    n_y = lax.axis_size("yz") * depth_y
    parts = (field_e, field_h, permittivity, conductivity[None])
    x_inner, x_outer = swap_halos(
        jnp.concatenate([p[:, :HALO] for p in parts], 0),
        jnp.concatenate([p[:, depth_x - HALO :] for p in parts], 0),
        "slab",
    )
    xlo, xhi = low_high(x_inner, x_outer, lax.axis_index("slab") % 2 == 1)
    def rows(start):
        center = jnp.concatenate([p[:, :, start : start + HALO] for p in parts], 0)
        return jnp.concatenate([center, xhi[:, :, start : start + HALO], xlo[:, :, start : start + HALO]], 1)

    y_inner, y_outer = swap_halos(rows(0), rows(depth_y - HALO), "yz")
    new_e, new_h, products = leapfrog(
        field_e, field_h, permittivity, conductivity[None], x_inner, x_outer, y_inner, y_outer,
        slot_cell[0, 0], jnp.transpose(forward_e[0, 0], (1, 0, 2)), n_x, n_y,
    )
    products = products.reshape(STEPS, sources, capacity)
    segments = recv_param.reshape(sources, capacity)
    if sources & (sources - 1) == 0:
        received, segments = exchange_by_halving(products, segments, sources)
    else:
        received = lax.all_to_all(products, "slab", split_axis=1, concat_axis=1, tiled=True)
    segments = jnp.broadcast_to(segments[None], received.shape).reshape(-1, 1)
    params = lax.broadcasted_iota(jnp.int32, (1, PAR_DEV), 1)
    gradient = jnp.sum(jnp.where(segments == params, received.reshape(-1, 1), 0.0), axis=0)
    return (new_e, new_h, gradient.reshape(1, 1, PAR_DEV))


def solution(mesh):
    return jax.shard_map(
        shards,
        mesh=mesh,
        in_specs=(
            P(None, "slab", "yz", None),
            P(None, "slab", "yz", None),
            P(None, "slab", "yz", None),
            P("slab", "yz", None),
            P("slab", "yz", None, None, None),
            P("slab", "yz", None, None),
            P("slab", "yz", None, None),
        ),
        out_specs=(P(None, "slab", "yz", None), P(None, "slab", "yz", None), P("slab", "yz", None)),
        check_vma=False,
    )
```

```python
import functools

import jax
import jax.numpy as jnp
from jax import lax
from jax.experimental import pallas as pl
from jax.experimental.pallas import tpu as pltpu
from jax.sharding import PartitionSpec as P

STEPS = 2
PAR_DEV = 128
HALO = 2
LANES = 128
RADIX = 4

CH_GAIN = 0.5
CE_GAIN = 0.5


def recv_from(array, axis, offset):
    count = lax.axis_size(axis)
    pairs = [(i + offset, i) for i in range(count) if 0 <= i + offset < count]
    return lax.ppermute(array, axis, pairs)


def ahead(values, axis):
    extent = values.shape[axis]
    if axis == 0:
        return jnp.concatenate([values[1:], values[:1]], 0)
    shifted = pltpu.roll(values, extent - 1, axis)
    if axis == 2:
        lane = lax.broadcasted_iota(jnp.int32, values.shape, 2)
        shifted = jnp.where(lane == extent - 1, 0.0, shifted)
    return shifted


def behind(values, axis):
    extent = values.shape[axis]
    if axis == 0:
        return jnp.concatenate([values[extent - 1 :], values[: extent - 1]], 0)
    shifted = pltpu.roll(values, 1, axis)
    if axis == 2:
        lane = lax.broadcasted_iota(jnp.int32, values.shape, 2)
        shifted = jnp.where(lane == 0, 0.0, shifted)
    return shifted


def swap_halos(first, last, axis):
    count = lax.axis_size(axis)
    odd = lax.axis_index(axis) % 2 == 1
    inner = [(i, i ^ 1) for i in range(count) if i ^ 1 < count]
    outer = [p for i in range(1, count - 1, 2) for p in ((i, i + 1), (i + 1, i))]
    got_inner = lax.ppermute(jnp.where(odd, first, last), axis, inner)
    got_outer = lax.ppermute(jnp.where(odd, last, first), axis, outer)
    return got_inner, got_outer


def low_high(got_inner, got_outer, odd):
    return jnp.where(odd, got_inner, got_outer), jnp.where(odd, got_outer, got_inner)


def leapfrog_kernel(
    dims, e_ref, h_ref, perm_ref, cond_ref, x_inner_ref, x_outer_ref, y_inner_ref, y_outer_ref,
    cell_ref, fwd_ref, e_out, h_out, prod_out, ring,
):
    depth_x, depth_y, n_x, n_y = dims
    ring_x, ring_y = ring.shape[1], ring.shape[2]
    slab, yz = lax.axis_index("slab"), lax.axis_index("yz")
    xlo, xhi = low_high(x_inner_ref[...], x_outer_ref[...], slab % 2 == 1)
    ylo, yhi = low_high(y_inner_ref[...], y_outer_ref[...], yz % 2 == 1)
    ring[0:3, 0:depth_x, 0:depth_y] = e_ref[...]
    ring[3:6, 0:depth_x, 0:depth_y] = h_ref[...]
    ring[6:9, 0:depth_x, 0:depth_y] = perm_ref[...]
    ring[9:10, 0:depth_x, 0:depth_y] = cond_ref[...]
    ring[:, depth_x : depth_x + HALO, 0:depth_y] = xhi
    ring[:, ring_x - HALO : ring_x, 0:depth_y] = xlo
    ring[:, :, depth_y : depth_y + HALO] = yhi
    ring[:, :, depth_y + HALO : ring_y - HALO] = jnp.zeros(
        (ring.shape[0], ring_x, ring_y - depth_y - 2 * HALO, LANES), jnp.float32
    )
    ring[:, :, ring_y - HALO : ring_y] = ylo

    shape = (ring_x, ring_y, LANES)
    xi = lax.broadcasted_iota(jnp.int32, shape, 0)
    yi = lax.broadcasted_iota(jnp.int32, shape, 1)
    gx = slab * depth_x + jnp.where(xi < depth_x + HALO, xi, xi - ring_x)
    gy = yz * depth_y + jnp.where(yi < depth_y + HALO, yi, yi - ring_y)
    y_real = (yi < depth_y + HALO) | (yi >= ring_y - HALO)
    inside = (gx >= 0) & (gx < n_x) & (gy >= 0) & (gy < n_y) & y_real

    field_e = [ring[c] for c in range(3)]
    field_h = [ring[3 + c] for c in range(3)]
    conductivity = ring[9]
    keep_rate, curl_gain = [], []
    half_loss = 0.5 * conductivity
    for c in range(3):
        permittivity = jnp.where(inside, ring[6 + c], 1.0)
        scale = 1.0 / (permittivity + half_loss)
        keep_rate.append((permittivity - half_loss) * scale)
        curl_gain.append(CE_GAIN * scale)

    grid = cell_ref[...].astype(jnp.float32)
    owners, capacity = grid.shape
    slots = owners * capacity
    slot = lax.broadcasted_iota(jnp.int32, (capacity, slots), 1)
    spread = (slot % capacity == lax.broadcasted_iota(jnp.int32, (capacity, slots), 0)).astype(jnp.float32)
    by_owner = jnp.dot(grid, spread, precision=lax.Precision.HIGHEST, preferred_element_type=jnp.float32)
    mine = lax.broadcasted_iota(jnp.int32, (owners, slots), 1) // capacity == lax.broadcasted_iota(
        jnp.int32, (owners, slots), 0
    )
    cells = jnp.sum(jnp.where(mine, by_owner, 0.0), axis=0, keepdims=True).astype(jnp.int32)
    rows = depth_x * depth_y
    lane_pick = (lax.broadcasted_iota(jnp.int32, (LANES, cells.shape[1]), 0) == (cells % LANES)).astype(jnp.float32)
    row_pick = lax.broadcasted_iota(jnp.int32, (rows, cells.shape[1]), 0) == (cells // LANES)

    blocks = []
    for step_index in range(STEPS):
        e0, e1, e2 = field_e
        curl = (
            (ahead(e2, 1) - e2) - (ahead(e1, 2) - e1),
            (ahead(e0, 2) - e0) - (ahead(e2, 0) - e2),
            (ahead(e1, 0) - e1) - (ahead(e0, 1) - e0),
        )
        field_h = [jnp.where(inside, field_h[c] - CH_GAIN * curl[c], 0.0) for c in range(3)]
        h0, h1, h2 = field_h
        curl = (
            (h2 - behind(h2, 1)) - (h1 - behind(h1, 2)),
            (h0 - behind(h0, 2)) - (h2 - behind(h2, 0)),
            (h1 - behind(h1, 0)) - (h0 - behind(h0, 1)),
        )
        field_e = [
            jnp.where(inside, keep_rate[c] * field_e[c] + curl_gain[c] * curl[c], 0.0) for c in range(3)
        ]
        blocks.extend(field_e[c][0:depth_x, 0:depth_y].reshape(rows, LANES) for c in range(3))

    by_lane = jnp.dot(
        jnp.concatenate(blocks, 0), lane_pick, precision=lax.Precision.HIGHEST, preferred_element_type=jnp.float32
    )
    for step_index in range(STEPS):
        product = None
        for c in range(3):
            part = by_lane[(3 * step_index + c) * rows : (3 * step_index + c + 1) * rows]
            picked = jnp.sum(jnp.where(row_pick, part, 0.0), axis=0, keepdims=True)
            term = picked * fwd_ref[c, step_index : step_index + 1, :]
            product = term if product is None else product + term
        prod_out[step_index : step_index + 1, :] = product

    for c in range(3):
        e_out[c] = field_e[c][0:depth_x, 0:depth_y]
        h_out[c] = field_h[c][0:depth_x, 0:depth_y]


def leapfrog(field_e, field_h, permittivity, conductivity, xlo, xhi, ylo, yhi, cells, fwd, n_x, n_y):
    _, depth_x, depth_y, _ = field_e.shape
    ring_x = depth_x + 2 * HALO
    ring_y = -(-(depth_y + 2 * HALO) // 8) * 8
    vmem = pl.BlockSpec(memory_space=pltpu.VMEM)
    kernel = functools.partial(leapfrog_kernel, (depth_x, depth_y, n_x, n_y))
    return pl.pallas_call(
        kernel,
        out_shape=(
            jax.ShapeDtypeStruct(field_e.shape, jnp.float32),
            jax.ShapeDtypeStruct(field_h.shape, jnp.float32),
            jax.ShapeDtypeStruct((STEPS, cells.size), jnp.float32),
        ),
        in_specs=[vmem] * 10,
        out_specs=(vmem, vmem, vmem),
        scratch_shapes=[pltpu.VMEM((10, ring_x, ring_y, LANES), jnp.float32)],
    )(field_e, field_h, permittivity, conductivity, xlo, xhi, ylo, yhi, cells, fwd)


def xor_rows(array, me, count, axis):
    bit = 1
    while bit < count:
        shape = array.shape[:axis] + (count // (2 * bit), 2, bit) + array.shape[axis + 1 :]
        split = array.reshape(shape)
        swapped = jnp.flip(split, axis + 1).reshape(array.shape)
        array = jnp.where((me // bit) % 2 == 1, swapped, array)
        bit *= 2
    return array


def exchange_by_halving(products, segments, count):
    me = lax.axis_index("slab")
    held = xor_rows(products, me, count, 1)[:, :, None]
    bit = count // 2
    while bit >= RADIX:
        owners = held.shape[1]
        keep = held[:, : owners // 2]
        send = held[:, owners // 2 :]
        pairs = [(i, i ^ bit) for i in range(count)]
        got = lax.ppermute(send, "slab", pairs)
        held = jnp.stack([keep, got], 3).reshape(keep.shape[:2] + (keep.shape[2] * 2,) + keep.shape[3:])
        bit //= 2
    owners = held.shape[1]
    pieces = [held[:, 0]]
    for q in range(1, owners):
        pieces.append(lax.ppermute(held[:, q], "slab", [(i, i ^ q) for i in range(count)]))
    held = jnp.stack(pieces, 2)
    held = held.reshape(held.shape[:1] + (held.shape[1] * owners,) + held.shape[3:])
    return held, xor_rows(segments, me, count, 0)


def shards(field_e, field_h, permittivity, conductivity, forward_e, slot_cell, recv_param):
    depth_x = field_e.shape[1]
    depth_y = field_e.shape[2]
    sources = recv_param.shape[2]
    capacity = recv_param.shape[3]
    n_x = lax.axis_size("slab") * depth_x
    n_y = lax.axis_size("yz") * depth_y
    parts = (field_e, field_h, permittivity, conductivity[None])
    x_inner, x_outer = swap_halos(
        jnp.concatenate([p[:, :HALO] for p in parts], 0),
        jnp.concatenate([p[:, depth_x - HALO :] for p in parts], 0),
        "slab",
    )
    xlo, xhi = low_high(x_inner, x_outer, lax.axis_index("slab") % 2 == 1)
    def rows(start):
        center = jnp.concatenate([p[:, :, start : start + HALO] for p in parts], 0)
        return jnp.concatenate([center, xhi[:, :, start : start + HALO], xlo[:, :, start : start + HALO]], 1)

    y_inner, y_outer = swap_halos(rows(0), rows(depth_y - HALO), "yz")
    new_e, new_h, products = leapfrog(
        field_e, field_h, permittivity, conductivity[None], x_inner, x_outer, y_inner, y_outer,
        slot_cell[0, 0], jnp.transpose(forward_e[0, 0], (1, 0, 2)), n_x, n_y,
    )
    products = products.reshape(STEPS, sources, capacity)
    segments = recv_param.reshape(sources, capacity)
    if sources & (sources - 1) == 0:
        received, segments = exchange_by_halving(products, segments, sources)
    else:
        received = lax.all_to_all(products, "slab", split_axis=1, concat_axis=1, tiled=True)
    segments = jnp.broadcast_to(segments[None], received.shape).reshape(-1, 1)
    params = lax.broadcasted_iota(jnp.int32, (1, PAR_DEV), 1)
    gradient = jnp.sum(jnp.where(segments == params, received.reshape(-1, 1), 0.0), axis=0)
    return (new_e, new_h, gradient.reshape(1, 1, PAR_DEV))


def solution(mesh):
    return jax.shard_map(
        shards,
        mesh=mesh,
        in_specs=(
            P(None, "slab", "yz", None),
            P(None, "slab", "yz", None),
            P(None, "slab", "yz", None),
            P("slab", "yz", None),
            P("slab", "yz", None, None, None),
            P("slab", "yz", None, None),
            P("slab", "yz", None, None),
        ),
        out_specs=(P(None, "slab", "yz", None), P(None, "slab", "yz", None), P("slab", "yz", None)),
        check_vma=False,
    )
```

```python
import functools

import jax
import jax.numpy as jnp
from jax import lax
from jax.experimental import pallas as pl
from jax.experimental.pallas import tpu as pltpu
from jax.sharding import PartitionSpec as P

STEPS = 2
PAR_DEV = 128
HALO = 2
LANES = 128
RADIX = 4

CH_GAIN = 0.5
CE_GAIN = 0.5


def recv_from(array, axis, offset):
    count = lax.axis_size(axis)
    pairs = [(i + offset, i) for i in range(count) if 0 <= i + offset < count]
    return lax.ppermute(array, axis, pairs)


def ahead(values, axis):
    extent = values.shape[axis]
    if axis == 0:
        return jnp.concatenate([values[1:], values[:1]], 0)
    shifted = pltpu.roll(values, extent - 1, axis)
    if axis == 2:
        lane = lax.broadcasted_iota(jnp.int32, values.shape, 2)
        shifted = jnp.where(lane == extent - 1, 0.0, shifted)
    return shifted


def behind(values, axis):
    extent = values.shape[axis]
    if axis == 0:
        return jnp.concatenate([values[extent - 1 :], values[: extent - 1]], 0)
    shifted = pltpu.roll(values, 1, axis)
    if axis == 2:
        lane = lax.broadcasted_iota(jnp.int32, values.shape, 2)
        shifted = jnp.where(lane == 0, 0.0, shifted)
    return shifted


def swap_halos(first, last, axis):
    count = lax.axis_size(axis)
    odd = lax.axis_index(axis) % 2 == 1
    inner = [(i, i ^ 1) for i in range(count) if i ^ 1 < count]
    outer = [p for i in range(1, count - 1, 2) for p in ((i, i + 1), (i + 1, i))]
    got_inner = lax.ppermute(jnp.where(odd, first, last), axis, inner)
    got_outer = lax.ppermute(jnp.where(odd, last, first), axis, outer)
    return got_inner, got_outer


def low_high(got_inner, got_outer, odd):
    return jnp.where(odd, got_inner, got_outer), jnp.where(odd, got_outer, got_inner)


def leapfrog_kernel(
    dims, e_ref, h_ref, perm_ref, cond_ref, x_inner_ref, x_outer_ref, y_inner_ref, y_outer_ref,
    cell_ref, fwd_ref, e_out, h_out, prod_out, ring,
):
    depth_x, depth_y, n_x, n_y = dims
    ring_x, ring_y = ring.shape[1], ring.shape[2]
    slab, yz = lax.axis_index("slab"), lax.axis_index("yz")
    xlo, xhi = low_high(x_inner_ref[...], x_outer_ref[...], slab % 2 == 1)
    ylo, yhi = low_high(y_inner_ref[...], y_outer_ref[...], yz % 2 == 1)
    ring[0:3, 0:depth_x, 0:depth_y] = e_ref[...]
    ring[3:6, 0:depth_x, 0:depth_y] = h_ref[...]
    ring[6:9, 0:depth_x, 0:depth_y] = perm_ref[...]
    ring[9:10, 0:depth_x, 0:depth_y] = cond_ref[...]
    ring[:, depth_x : depth_x + HALO, 0:depth_y] = xhi
    ring[:, ring_x - HALO : ring_x, 0:depth_y] = xlo
    ring[:, :, depth_y : depth_y + HALO] = yhi
    ring[:, :, depth_y + HALO : ring_y - HALO] = jnp.zeros(
        (ring.shape[0], ring_x, ring_y - depth_y - 2 * HALO, LANES), jnp.float32
    )
    ring[:, :, ring_y - HALO : ring_y] = ylo

    shape = (ring_x, ring_y, LANES)
    xi = lax.broadcasted_iota(jnp.int32, shape, 0)
    yi = lax.broadcasted_iota(jnp.int32, shape, 1)
    gx = slab * depth_x + jnp.where(xi < depth_x + HALO, xi, xi - ring_x)
    gy = yz * depth_y + jnp.where(yi < depth_y + HALO, yi, yi - ring_y)
    y_real = (yi < depth_y + HALO) | (yi >= ring_y - HALO)
    inside = (gx >= 0) & (gx < n_x) & (gy >= 0) & (gy < n_y) & y_real

    field_e = [ring[c] for c in range(3)]
    field_h = [ring[3 + c] for c in range(3)]
    conductivity = ring[9]
    keep_rate, curl_gain = [], []
    for c in range(3):
        permittivity = jnp.where(inside, ring[6 + c], 1.0)
        ratio = 0.5 * conductivity / permittivity
        keep_rate.append((1.0 - ratio) / (1.0 + ratio))
        curl_gain.append(CE_GAIN / (permittivity * (1.0 + ratio)))

    grid = cell_ref[...].astype(jnp.float32)
    owners, capacity = grid.shape
    slots = owners * capacity
    slot = lax.broadcasted_iota(jnp.int32, (capacity, slots), 1)
    spread = (slot % capacity == lax.broadcasted_iota(jnp.int32, (capacity, slots), 0)).astype(jnp.float32)
    by_owner = jnp.dot(grid, spread, precision=lax.Precision.HIGHEST, preferred_element_type=jnp.float32)
    mine = lax.broadcasted_iota(jnp.int32, (owners, slots), 1) // capacity == lax.broadcasted_iota(
        jnp.int32, (owners, slots), 0
    )
    cells = jnp.sum(jnp.where(mine, by_owner, 0.0), axis=0, keepdims=True).astype(jnp.int32)
    rows = depth_x * depth_y
    lane_pick = (lax.broadcasted_iota(jnp.int32, (LANES, cells.shape[1]), 0) == (cells % LANES)).astype(jnp.float32)
    row_pick = lax.broadcasted_iota(jnp.int32, (rows, cells.shape[1]), 0) == (cells // LANES)

    for step_index in range(STEPS):
        e0, e1, e2 = field_e
        curl = (
            (ahead(e2, 1) - e2) - (ahead(e1, 2) - e1),
            (ahead(e0, 2) - e0) - (ahead(e2, 0) - e2),
            (ahead(e1, 0) - e1) - (ahead(e0, 1) - e0),
        )
        field_h = [jnp.where(inside, field_h[c] - CH_GAIN * curl[c], 0.0) for c in range(3)]
        h0, h1, h2 = field_h
        curl = (
            (h2 - behind(h2, 1)) - (h1 - behind(h1, 2)),
            (h0 - behind(h0, 2)) - (h2 - behind(h2, 0)),
            (h1 - behind(h1, 0)) - (h0 - behind(h0, 1)),
        )
        field_e = [
            jnp.where(inside, keep_rate[c] * field_e[c] + curl_gain[c] * curl[c], 0.0) for c in range(3)
        ]
        product = None
        for c in range(3):
            block = field_e[c][0:depth_x, 0:depth_y].reshape(rows, LANES)
            by_lane = jnp.dot(block, lane_pick, precision=lax.Precision.HIGHEST, preferred_element_type=jnp.float32)
            picked = jnp.sum(jnp.where(row_pick, by_lane, 0.0), axis=0, keepdims=True)
            term = picked * fwd_ref[c, step_index : step_index + 1, :]
            product = term if product is None else product + term
        if owners & (owners - 1):
            prod_out[step_index : step_index + 1, :] = product
            continue
        target = lax.broadcasted_iota(jnp.int32, (slots, slots), 1)
        source = (jnp.bitwise_xor(target // capacity, slab)) * capacity + target % capacity
        move = (lax.broadcasted_iota(jnp.int32, (slots, slots), 0) == source).astype(jnp.float32)
        prod_out[step_index : step_index + 1, :] = jnp.dot(
            product, move, precision=lax.Precision.HIGHEST, preferred_element_type=jnp.float32
        )

    for c in range(3):
        e_out[c] = field_e[c][0:depth_x, 0:depth_y]
        h_out[c] = field_h[c][0:depth_x, 0:depth_y]


def leapfrog(field_e, field_h, permittivity, conductivity, xlo, xhi, ylo, yhi, cells, fwd, n_x, n_y):
    _, depth_x, depth_y, _ = field_e.shape
    ring_x = depth_x + 2 * HALO
    ring_y = -(-(depth_y + 2 * HALO) // 8) * 8
    vmem = pl.BlockSpec(memory_space=pltpu.VMEM)
    kernel = functools.partial(leapfrog_kernel, (depth_x, depth_y, n_x, n_y))
    return pl.pallas_call(
        kernel,
        out_shape=(
            jax.ShapeDtypeStruct(field_e.shape, jnp.float32),
            jax.ShapeDtypeStruct(field_h.shape, jnp.float32),
            jax.ShapeDtypeStruct((STEPS, cells.size), jnp.float32),
        ),
        in_specs=[vmem] * 10,
        out_specs=(vmem, vmem, vmem),
        scratch_shapes=[pltpu.VMEM((10, ring_x, ring_y, LANES), jnp.float32)],
    )(field_e, field_h, permittivity, conductivity, xlo, xhi, ylo, yhi, cells, fwd)


def xor_rows(array, me, count, axis):
    bit = 1
    while bit < count:
        shape = array.shape[:axis] + (count // (2 * bit), 2, bit) + array.shape[axis + 1 :]
        split = array.reshape(shape)
        swapped = jnp.flip(split, axis + 1).reshape(array.shape)
        array = jnp.where((me // bit) % 2 == 1, swapped, array)
        bit *= 2
    return array


def exchange_by_halving(products, segments, count):
    me = lax.axis_index("slab")
    held = products[:, :, None]
    bit = count // 2
    while bit >= RADIX:
        owners = held.shape[1]
        keep = held[:, : owners // 2]
        send = held[:, owners // 2 :]
        pairs = [(i, i ^ bit) for i in range(count)]
        got = lax.ppermute(send, "slab", pairs)
        held = jnp.stack([keep, got], 3).reshape(keep.shape[:2] + (keep.shape[2] * 2,) + keep.shape[3:])
        bit //= 2
    owners = held.shape[1]
    pieces = [held[:, 0]]
    for q in range(1, owners):
        pieces.append(lax.ppermute(held[:, q], "slab", [(i, i ^ q) for i in range(count)]))
    held = jnp.stack(pieces, 2)
    held = held.reshape(held.shape[:1] + (held.shape[1] * owners,) + held.shape[3:])
    return held, xor_rows(segments, me, count, 0)


def shards(field_e, field_h, permittivity, conductivity, forward_e, slot_cell, recv_param):
    depth_x = field_e.shape[1]
    depth_y = field_e.shape[2]
    sources = recv_param.shape[2]
    capacity = recv_param.shape[3]
    n_x = lax.axis_size("slab") * depth_x
    n_y = lax.axis_size("yz") * depth_y
    parts = (field_e, field_h, permittivity, conductivity[None])
    x_inner, x_outer = swap_halos(
        jnp.concatenate([p[:, :HALO] for p in parts], 0),
        jnp.concatenate([p[:, depth_x - HALO :] for p in parts], 0),
        "slab",
    )
    xlo, xhi = low_high(x_inner, x_outer, lax.axis_index("slab") % 2 == 1)
    def rows(start):
        center = jnp.concatenate([p[:, :, start : start + HALO] for p in parts], 0)
        return jnp.concatenate([center, xhi[:, :, start : start + HALO], xlo[:, :, start : start + HALO]], 1)

    y_inner, y_outer = swap_halos(rows(0), rows(depth_y - HALO), "yz")
    new_e, new_h, products = leapfrog(
        field_e, field_h, permittivity, conductivity[None], x_inner, x_outer, y_inner, y_outer,
        slot_cell[0, 0], jnp.transpose(forward_e[0, 0], (1, 0, 2)), n_x, n_y,
    )
    products = products.reshape(STEPS, sources, capacity)
    segments = recv_param.reshape(sources, capacity)
    if sources & (sources - 1) == 0:
        received, segments = exchange_by_halving(products, segments, sources)
    else:
        received = lax.all_to_all(products, "slab", split_axis=1, concat_axis=1, tiled=True)
    segments = jnp.broadcast_to(segments[None], received.shape).reshape(-1, 1)
    params = lax.broadcasted_iota(jnp.int32, (1, PAR_DEV), 1)
    gradient = jnp.sum(jnp.where(segments == params, received.reshape(-1, 1), 0.0), axis=0)
    return (new_e, new_h, gradient.reshape(1, 1, PAR_DEV))


def solution(mesh):
    return jax.shard_map(
        shards,
        mesh=mesh,
        in_specs=(
            P(None, "slab", "yz", None),
            P(None, "slab", "yz", None),
            P(None, "slab", "yz", None),
            P("slab", "yz", None),
            P("slab", "yz", None, None, None),
            P("slab", "yz", None, None),
            P("slab", "yz", None, None),
        ),
        out_specs=(P(None, "slab", "yz", None), P(None, "slab", "yz", None), P("slab", "yz", None)),
        check_vma=False,
    )
```

```python
import functools

import jax
import jax.numpy as jnp
from jax import lax
from jax.experimental import pallas as pl
from jax.experimental.pallas import tpu as pltpu
from jax.sharding import PartitionSpec as P

STEPS = 2
PAR_DEV = 128
HALO = 2
LANES = 128
RADIX = 4

CH_GAIN = 0.5
CE_GAIN = 0.5


def recv_from(array, axis, offset):
    count = lax.axis_size(axis)
    pairs = [(i + offset, i) for i in range(count) if 0 <= i + offset < count]
    return lax.ppermute(array, axis, pairs)


def ahead(values, axis):
    extent = values.shape[axis]
    if axis == 0:
        return jnp.concatenate([values[1:], values[:1]], 0)
    shifted = pltpu.roll(values, extent - 1, axis)
    if axis == 2:
        lane = lax.broadcasted_iota(jnp.int32, values.shape, 2)
        shifted = jnp.where(lane == extent - 1, 0.0, shifted)
    return shifted


def behind(values, axis):
    extent = values.shape[axis]
    if axis == 0:
        return jnp.concatenate([values[extent - 1 :], values[: extent - 1]], 0)
    shifted = pltpu.roll(values, 1, axis)
    if axis == 2:
        lane = lax.broadcasted_iota(jnp.int32, values.shape, 2)
        shifted = jnp.where(lane == 0, 0.0, shifted)
    return shifted


def swap_halos(first, last, axis):
    count = lax.axis_size(axis)
    odd = lax.axis_index(axis) % 2 == 1
    inner = [(i, i ^ 1) for i in range(count) if i ^ 1 < count]
    outer = [p for i in range(1, count - 1, 2) for p in ((i, i + 1), (i + 1, i))]
    got_inner = lax.ppermute(jnp.where(odd, first, last), axis, inner)
    got_outer = lax.ppermute(jnp.where(odd, last, first), axis, outer)
    return got_inner, got_outer


def low_high(got_inner, got_outer, odd):
    return jnp.where(odd, got_inner, got_outer), jnp.where(odd, got_outer, got_inner)


def pack_kernel(e_ref, h_ref, perm_ref, cond_ref, inner_ref, outer_ref, sems):
    depth_x = e_ref.shape[1]
    odd = lax.axis_index("slab") % 2
    inner = (1 - odd) * (depth_x - HALO)
    outer = odd * (depth_x - HALO)
    copies = []
    for out_ref, start in ((inner_ref, inner), (outer_ref, outer)):
        planes = pl.ds(start, HALO)
        for lo, src in ((0, e_ref), (3, h_ref), (6, perm_ref)):
            copies.append((src.at[:, planes], out_ref.at[lo : lo + 3]))
        copies.append((cond_ref.at[planes], out_ref.at[9]))
    started = [pltpu.make_async_copy(a, b, sems.at[i]) for i, (a, b) in enumerate(copies)]
    for copy in started:
        copy.start()
    for copy in started:
        copy.wait()


def pack_x_halos(field_e, field_h, permittivity, conductivity):
    _, depth_x, depth_y, lanes = field_e.shape
    anywhere = pl.BlockSpec(memory_space=pl.ANY)
    piece = jax.ShapeDtypeStruct((10, HALO, depth_y, lanes), jnp.float32)
    return pl.pallas_call(
        pack_kernel,
        out_shape=(piece, piece),
        in_specs=[anywhere] * 4,
        out_specs=(anywhere, anywhere),
        scratch_shapes=[pltpu.SemaphoreType.DMA((8,))],
    )(field_e, field_h, permittivity, conductivity)


def leapfrog_kernel(
    dims, e_ref, h_ref, perm_ref, cond_ref, x_inner_ref, x_outer_ref, y_inner_ref, y_outer_ref,
    cell_ref, fwd_ref, e_out, h_out, prod_out, ring,
):
    depth_x, depth_y, n_x, n_y = dims
    ring_x, ring_y = ring.shape[1], ring.shape[2]
    slab, yz = lax.axis_index("slab"), lax.axis_index("yz")
    xlo, xhi = low_high(x_inner_ref[...], x_outer_ref[...], slab % 2 == 1)
    ylo, yhi = low_high(y_inner_ref[...], y_outer_ref[...], yz % 2 == 1)
    ring[0:3, 0:depth_x, 0:depth_y] = e_ref[...]
    ring[3:6, 0:depth_x, 0:depth_y] = h_ref[...]
    ring[6:9, 0:depth_x, 0:depth_y] = perm_ref[...]
    ring[9:10, 0:depth_x, 0:depth_y] = cond_ref[...]
    ring[:, depth_x : depth_x + HALO, 0:depth_y] = xhi
    ring[:, ring_x - HALO : ring_x, 0:depth_y] = xlo
    ring[:, :, depth_y : depth_y + HALO] = yhi
    ring[:, :, depth_y + HALO : ring_y - HALO] = jnp.zeros(
        (ring.shape[0], ring_x, ring_y - depth_y - 2 * HALO, LANES), jnp.float32
    )
    ring[:, :, ring_y - HALO : ring_y] = ylo

    shape = (ring_x, ring_y, LANES)
    xi = lax.broadcasted_iota(jnp.int32, shape, 0)
    yi = lax.broadcasted_iota(jnp.int32, shape, 1)
    gx = slab * depth_x + jnp.where(xi < depth_x + HALO, xi, xi - ring_x)
    gy = yz * depth_y + jnp.where(yi < depth_y + HALO, yi, yi - ring_y)
    y_real = (yi < depth_y + HALO) | (yi >= ring_y - HALO)
    inside = (gx >= 0) & (gx < n_x) & (gy >= 0) & (gy < n_y) & y_real

    field_e = [ring[c] for c in range(3)]
    field_h = [ring[3 + c] for c in range(3)]
    conductivity = ring[9]
    keep_rate, curl_gain = [], []
    for c in range(3):
        permittivity = jnp.where(inside, ring[6 + c], 1.0)
        ratio = 0.5 * conductivity / permittivity
        keep_rate.append((1.0 - ratio) / (1.0 + ratio))
        curl_gain.append(CE_GAIN / (permittivity * (1.0 + ratio)))

    grid = cell_ref[...].astype(jnp.float32)
    owners, capacity = grid.shape
    slots = owners * capacity
    slot = lax.broadcasted_iota(jnp.int32, (capacity, slots), 1)
    spread = (slot % capacity == lax.broadcasted_iota(jnp.int32, (capacity, slots), 0)).astype(jnp.float32)
    by_owner = jnp.dot(grid, spread, precision=lax.Precision.HIGHEST, preferred_element_type=jnp.float32)
    mine = lax.broadcasted_iota(jnp.int32, (owners, slots), 1) // capacity == lax.broadcasted_iota(
        jnp.int32, (owners, slots), 0
    )
    cells = jnp.sum(jnp.where(mine, by_owner, 0.0), axis=0, keepdims=True).astype(jnp.int32)
    rows = depth_x * depth_y
    lane_pick = (lax.broadcasted_iota(jnp.int32, (LANES, cells.shape[1]), 0) == (cells % LANES)).astype(jnp.float32)
    row_pick = lax.broadcasted_iota(jnp.int32, (rows, cells.shape[1]), 0) == (cells // LANES)

    for step_index in range(STEPS):
        e0, e1, e2 = field_e
        curl = (
            (ahead(e2, 1) - e2) - (ahead(e1, 2) - e1),
            (ahead(e0, 2) - e0) - (ahead(e2, 0) - e2),
            (ahead(e1, 0) - e1) - (ahead(e0, 1) - e0),
        )
        field_h = [jnp.where(inside, field_h[c] - CH_GAIN * curl[c], 0.0) for c in range(3)]
        h0, h1, h2 = field_h
        curl = (
            (h2 - behind(h2, 1)) - (h1 - behind(h1, 2)),
            (h0 - behind(h0, 2)) - (h2 - behind(h2, 0)),
            (h1 - behind(h1, 0)) - (h0 - behind(h0, 1)),
        )
        field_e = [
            jnp.where(inside, keep_rate[c] * field_e[c] + curl_gain[c] * curl[c], 0.0) for c in range(3)
        ]
        product = None
        for c in range(3):
            block = field_e[c][0:depth_x, 0:depth_y].reshape(rows, LANES)
            by_lane = jnp.dot(block, lane_pick, precision=lax.Precision.HIGHEST, preferred_element_type=jnp.float32)
            picked = jnp.sum(jnp.where(row_pick, by_lane, 0.0), axis=0, keepdims=True)
            term = picked * fwd_ref[c, step_index : step_index + 1, :]
            product = term if product is None else product + term
        prod_out[step_index : step_index + 1, :] = product

    for c in range(3):
        e_out[c] = field_e[c][0:depth_x, 0:depth_y]
        h_out[c] = field_h[c][0:depth_x, 0:depth_y]


def leapfrog(field_e, field_h, permittivity, conductivity, xlo, xhi, ylo, yhi, cells, fwd, n_x, n_y):
    _, depth_x, depth_y, _ = field_e.shape
    ring_x = depth_x + 2 * HALO
    ring_y = -(-(depth_y + 2 * HALO) // 8) * 8
    vmem = pl.BlockSpec(memory_space=pltpu.VMEM)
    kernel = functools.partial(leapfrog_kernel, (depth_x, depth_y, n_x, n_y))
    return pl.pallas_call(
        kernel,
        out_shape=(
            jax.ShapeDtypeStruct(field_e.shape, jnp.float32),
            jax.ShapeDtypeStruct(field_h.shape, jnp.float32),
            jax.ShapeDtypeStruct((STEPS, cells.size), jnp.float32),
        ),
        in_specs=[vmem] * 10,
        out_specs=(vmem, vmem, vmem),
        scratch_shapes=[pltpu.VMEM((10, ring_x, ring_y, LANES), jnp.float32)],
    )(field_e, field_h, permittivity, conductivity, xlo, xhi, ylo, yhi, cells, fwd)


def xor_rows(array, me, count, axis):
    bit = 1
    while bit < count:
        shape = array.shape[:axis] + (count // (2 * bit), 2, bit) + array.shape[axis + 1 :]
        split = array.reshape(shape)
        swapped = jnp.flip(split, axis + 1).reshape(array.shape)
        array = jnp.where((me // bit) % 2 == 1, swapped, array)
        bit *= 2
    return array


def exchange_by_halving(products, segments, count):
    me = lax.axis_index("slab")
    held = xor_rows(products, me, count, 1)[:, :, None]
    bit = count // 2
    while bit >= RADIX:
        owners = held.shape[1]
        keep = held[:, : owners // 2]
        send = held[:, owners // 2 :]
        pairs = [(i, i ^ bit) for i in range(count)]
        got = lax.ppermute(send, "slab", pairs)
        held = jnp.stack([keep, got], 3).reshape(keep.shape[:2] + (keep.shape[2] * 2,) + keep.shape[3:])
        bit //= 2
    owners = held.shape[1]
    pieces = [held[:, 0]]
    for q in range(1, owners):
        pieces.append(lax.ppermute(held[:, q], "slab", [(i, i ^ q) for i in range(count)]))
    held = jnp.stack(pieces, 2)
    held = held.reshape(held.shape[:1] + (held.shape[1] * owners,) + held.shape[3:])
    return held, xor_rows(segments, me, count, 0)


def shards(field_e, field_h, permittivity, conductivity, forward_e, slot_cell, recv_param):
    depth_x = field_e.shape[1]
    depth_y = field_e.shape[2]
    sources = recv_param.shape[2]
    capacity = recv_param.shape[3]
    n_x = lax.axis_size("slab") * depth_x
    n_y = lax.axis_size("yz") * depth_y
    parts = (field_e, field_h, permittivity, conductivity[None])
    send_inner, send_outer = pack_x_halos(field_e, field_h, permittivity, conductivity)
    count = lax.axis_size("slab")
    x_inner = lax.ppermute(send_inner, "slab", [(i, i ^ 1) for i in range(count) if i ^ 1 < count])
    x_outer = lax.ppermute(
        send_outer, "slab", [p for i in range(1, count - 1, 2) for p in ((i, i + 1), (i + 1, i))]
    )
    xlo, xhi = low_high(x_inner, x_outer, lax.axis_index("slab") % 2 == 1)
    def rows(start):
        center = jnp.concatenate([p[:, :, start : start + HALO] for p in parts], 0)
        return jnp.concatenate([center, xhi[:, :, start : start + HALO], xlo[:, :, start : start + HALO]], 1)

    y_inner, y_outer = swap_halos(rows(0), rows(depth_y - HALO), "yz")
    new_e, new_h, products = leapfrog(
        field_e, field_h, permittivity, conductivity[None], x_inner, x_outer, y_inner, y_outer,
        slot_cell[0, 0], jnp.transpose(forward_e[0, 0], (1, 0, 2)), n_x, n_y,
    )
    products = products.reshape(STEPS, sources, capacity)
    segments = recv_param.reshape(sources, capacity)
    if sources & (sources - 1) == 0:
        received, segments = exchange_by_halving(products, segments, sources)
    else:
        received = lax.all_to_all(products, "slab", split_axis=1, concat_axis=1, tiled=True)
    segments = jnp.broadcast_to(segments[None], received.shape).reshape(-1, 1)
    params = lax.broadcasted_iota(jnp.int32, (1, PAR_DEV), 1)
    gradient = jnp.sum(jnp.where(segments == params, received.reshape(-1, 1), 0.0), axis=0)
    return (new_e, new_h, gradient.reshape(1, 1, PAR_DEV))


def solution(mesh):
    return jax.shard_map(
        shards,
        mesh=mesh,
        in_specs=(
            P(None, "slab", "yz", None),
            P(None, "slab", "yz", None),
            P(None, "slab", "yz", None),
            P("slab", "yz", None),
            P("slab", "yz", None, None, None),
            P("slab", "yz", None, None),
            P("slab", "yz", None, None),
        ),
        out_specs=(P(None, "slab", "yz", None), P(None, "slab", "yz", None), P("slab", "yz", None)),
        check_vma=False,
    )
```

```python
import functools

import jax
import jax.numpy as jnp
from jax import lax
from jax.experimental import pallas as pl
from jax.experimental.pallas import tpu as pltpu
from jax.sharding import PartitionSpec as P

STEPS = 2
PAR_DEV = 128
HALO = 2
LANES = 128
RADIX = 4

CH_GAIN = 0.5
CE_GAIN = 0.5


def recv_from(array, axis, offset):
    count = lax.axis_size(axis)
    pairs = [(i + offset, i) for i in range(count) if 0 <= i + offset < count]
    return lax.ppermute(array, axis, pairs)


def ahead(values, axis):
    extent = values.shape[axis]
    if axis == 0:
        return jnp.concatenate([values[1:], values[:1]], 0)
    shifted = pltpu.roll(values, extent - 1, axis)
    if axis == 2:
        lane = lax.broadcasted_iota(jnp.int32, values.shape, 2)
        shifted = jnp.where(lane == extent - 1, 0.0, shifted)
    return shifted


def behind(values, axis):
    extent = values.shape[axis]
    if axis == 0:
        return jnp.concatenate([values[extent - 1 :], values[: extent - 1]], 0)
    shifted = pltpu.roll(values, 1, axis)
    if axis == 2:
        lane = lax.broadcasted_iota(jnp.int32, values.shape, 2)
        shifted = jnp.where(lane == 0, 0.0, shifted)
    return shifted


def swap_halos(first, last, axis):
    count = lax.axis_size(axis)
    odd = lax.axis_index(axis) % 2 == 1
    inner = [(i, i ^ 1) for i in range(count) if i ^ 1 < count]
    outer = [p for i in range(1, count - 1, 2) for p in ((i, i + 1), (i + 1, i))]
    got_inner = lax.ppermute(jnp.where(odd, first, last), axis, inner)
    got_outer = lax.ppermute(jnp.where(odd, last, first), axis, outer)
    return got_inner, got_outer


def low_high(got_inner, got_outer, odd):
    return jnp.where(odd, got_inner, got_outer), jnp.where(odd, got_outer, got_inner)


def pack_planes(parts, start, near):
    fields = [p[:, start : start + HALO].reshape((-1,) + p.shape[2:]) for p in parts[:2]]
    material = [parts[2][:, start + near], parts[3][:, start + near]]
    return jnp.concatenate(fields + material, 0)


def unpack_planes(piece, near):
    rows = piece.shape[1:]
    fields = piece[0:12].reshape((6, HALO) + rows)
    material = piece[12:16][:, None]
    filler = jnp.concatenate([jnp.ones((3, 1) + rows, jnp.float32), jnp.zeros((1, 1) + rows, jnp.float32)], 0)
    planes = [material, filler] if near == 0 else [filler, material]
    return jnp.concatenate([fields, jnp.concatenate(planes, 1)], 0)


def leapfrog_kernel(
    dims, e_ref, h_ref, perm_ref, cond_ref, x_inner_ref, x_outer_ref, y_inner_ref, y_outer_ref,
    cell_ref, fwd_ref, e_out, h_out, prod_out, ring,
):
    depth_x, depth_y, n_x, n_y = dims
    ring_x, ring_y = ring.shape[1], ring.shape[2]
    slab, yz = lax.axis_index("slab"), lax.axis_index("yz")
    xlo, xhi = low_high(x_inner_ref[...], x_outer_ref[...], slab % 2 == 1)
    xlo, xhi = unpack_planes(xlo, HALO - 1), unpack_planes(xhi, 0)
    ylo, yhi = low_high(y_inner_ref[...], y_outer_ref[...], yz % 2 == 1)
    ring[0:3, 0:depth_x, 0:depth_y] = e_ref[...]
    ring[3:6, 0:depth_x, 0:depth_y] = h_ref[...]
    ring[6:9, 0:depth_x, 0:depth_y] = perm_ref[...]
    ring[9:10, 0:depth_x, 0:depth_y] = cond_ref[...]
    ring[:, depth_x : depth_x + HALO, 0:depth_y] = xhi
    ring[:, ring_x - HALO : ring_x, 0:depth_y] = xlo
    ring[:, :, depth_y : depth_y + HALO] = yhi
    ring[:, :, depth_y + HALO : ring_y - HALO] = jnp.zeros(
        (ring.shape[0], ring_x, ring_y - depth_y - 2 * HALO, LANES), jnp.float32
    )
    ring[:, :, ring_y - HALO : ring_y] = ylo

    shape = (ring_x, ring_y, LANES)
    xi = lax.broadcasted_iota(jnp.int32, shape, 0)
    yi = lax.broadcasted_iota(jnp.int32, shape, 1)
    gx = slab * depth_x + jnp.where(xi < depth_x + HALO, xi, xi - ring_x)
    gy = yz * depth_y + jnp.where(yi < depth_y + HALO, yi, yi - ring_y)
    y_real = (yi < depth_y + HALO) | (yi >= ring_y - HALO)
    inside = (gx >= 0) & (gx < n_x) & (gy >= 0) & (gy < n_y) & y_real

    field_e = [ring[c] for c in range(3)]
    field_h = [ring[3 + c] for c in range(3)]
    conductivity = ring[9]
    keep_rate, curl_gain = [], []
    for c in range(3):
        permittivity = jnp.where(inside, ring[6 + c], 1.0)
        ratio = 0.5 * conductivity / permittivity
        keep_rate.append((1.0 - ratio) / (1.0 + ratio))
        curl_gain.append(CE_GAIN / (permittivity * (1.0 + ratio)))

    grid = cell_ref[...].astype(jnp.float32)
    owners, capacity = grid.shape
    slots = owners * capacity
    slot = lax.broadcasted_iota(jnp.int32, (capacity, slots), 1)
    spread = (slot % capacity == lax.broadcasted_iota(jnp.int32, (capacity, slots), 0)).astype(jnp.float32)
    by_owner = jnp.dot(grid, spread, precision=lax.Precision.HIGHEST, preferred_element_type=jnp.float32)
    mine = lax.broadcasted_iota(jnp.int32, (owners, slots), 1) // capacity == lax.broadcasted_iota(
        jnp.int32, (owners, slots), 0
    )
    cells = jnp.sum(jnp.where(mine, by_owner, 0.0), axis=0, keepdims=True).astype(jnp.int32)
    rows = depth_x * depth_y
    lane_pick = (lax.broadcasted_iota(jnp.int32, (LANES, cells.shape[1]), 0) == (cells % LANES)).astype(jnp.float32)
    row_pick = lax.broadcasted_iota(jnp.int32, (rows, cells.shape[1]), 0) == (cells // LANES)

    for step_index in range(STEPS):
        e0, e1, e2 = field_e
        curl = (
            (ahead(e2, 1) - e2) - (ahead(e1, 2) - e1),
            (ahead(e0, 2) - e0) - (ahead(e2, 0) - e2),
            (ahead(e1, 0) - e1) - (ahead(e0, 1) - e0),
        )
        field_h = [jnp.where(inside, field_h[c] - CH_GAIN * curl[c], 0.0) for c in range(3)]
        h0, h1, h2 = field_h
        curl = (
            (h2 - behind(h2, 1)) - (h1 - behind(h1, 2)),
            (h0 - behind(h0, 2)) - (h2 - behind(h2, 0)),
            (h1 - behind(h1, 0)) - (h0 - behind(h0, 1)),
        )
        field_e = [
            jnp.where(inside, keep_rate[c] * field_e[c] + curl_gain[c] * curl[c], 0.0) for c in range(3)
        ]
        product = None
        for c in range(3):
            block = field_e[c][0:depth_x, 0:depth_y].reshape(rows, LANES)
            by_lane = jnp.dot(block, lane_pick, precision=lax.Precision.HIGHEST, preferred_element_type=jnp.float32)
            picked = jnp.sum(jnp.where(row_pick, by_lane, 0.0), axis=0, keepdims=True)
            term = picked * fwd_ref[c, step_index : step_index + 1, :]
            product = term if product is None else product + term
        prod_out[step_index : step_index + 1, :] = product

    for c in range(3):
        e_out[c] = field_e[c][0:depth_x, 0:depth_y]
        h_out[c] = field_h[c][0:depth_x, 0:depth_y]


def leapfrog(field_e, field_h, permittivity, conductivity, xlo, xhi, ylo, yhi, cells, fwd, n_x, n_y):
    _, depth_x, depth_y, _ = field_e.shape
    ring_x = depth_x + 2 * HALO
    ring_y = -(-(depth_y + 2 * HALO) // 8) * 8
    vmem = pl.BlockSpec(memory_space=pltpu.VMEM)
    kernel = functools.partial(leapfrog_kernel, (depth_x, depth_y, n_x, n_y))
    return pl.pallas_call(
        kernel,
        out_shape=(
            jax.ShapeDtypeStruct(field_e.shape, jnp.float32),
            jax.ShapeDtypeStruct(field_h.shape, jnp.float32),
            jax.ShapeDtypeStruct((STEPS, cells.size), jnp.float32),
        ),
        in_specs=[vmem] * 10,
        out_specs=(vmem, vmem, vmem),
        scratch_shapes=[pltpu.VMEM((10, ring_x, ring_y, LANES), jnp.float32)],
    )(field_e, field_h, permittivity, conductivity, xlo, xhi, ylo, yhi, cells, fwd)


def xor_rows(array, me, count, axis):
    bit = 1
    while bit < count:
        shape = array.shape[:axis] + (count // (2 * bit), 2, bit) + array.shape[axis + 1 :]
        split = array.reshape(shape)
        swapped = jnp.flip(split, axis + 1).reshape(array.shape)
        array = jnp.where((me // bit) % 2 == 1, swapped, array)
        bit *= 2
    return array


def exchange_by_halving(products, segments, count):
    me = lax.axis_index("slab")
    held = xor_rows(products, me, count, 1)[:, :, None]
    bit = count // 2
    while bit >= RADIX:
        owners = held.shape[1]
        keep = held[:, : owners // 2]
        send = held[:, owners // 2 :]
        pairs = [(i, i ^ bit) for i in range(count)]
        got = lax.ppermute(send, "slab", pairs)
        held = jnp.stack([keep, got], 3).reshape(keep.shape[:2] + (keep.shape[2] * 2,) + keep.shape[3:])
        bit //= 2
    owners = held.shape[1]
    pieces = [held[:, 0]]
    for q in range(1, owners):
        pieces.append(lax.ppermute(held[:, q], "slab", [(i, i ^ q) for i in range(count)]))
    held = jnp.stack(pieces, 2)
    held = held.reshape(held.shape[:1] + (held.shape[1] * owners,) + held.shape[3:])
    return held, xor_rows(segments, me, count, 0)


def shards(field_e, field_h, permittivity, conductivity, forward_e, slot_cell, recv_param):
    depth_x = field_e.shape[1]
    depth_y = field_e.shape[2]
    sources = recv_param.shape[2]
    capacity = recv_param.shape[3]
    n_x = lax.axis_size("slab") * depth_x
    n_y = lax.axis_size("yz") * depth_y
    parts = (field_e, field_h, permittivity, conductivity[None])
    x_inner, x_outer = swap_halos(
        pack_planes(parts, 0, 0), pack_planes(parts, depth_x - HALO, HALO - 1), "slab"
    )
    xlo, xhi = low_high(x_inner, x_outer, lax.axis_index("slab") % 2 == 1)
    xlo, xhi = unpack_planes(xlo, HALO - 1), unpack_planes(xhi, 0)
    def rows(start):
        center = jnp.concatenate([p[:, :, start : start + HALO] for p in parts], 0)
        return jnp.concatenate([center, xhi[:, :, start : start + HALO], xlo[:, :, start : start + HALO]], 1)

    y_inner, y_outer = swap_halos(rows(0), rows(depth_y - HALO), "yz")
    new_e, new_h, products = leapfrog(
        field_e, field_h, permittivity, conductivity[None], x_inner, x_outer, y_inner, y_outer,
        slot_cell[0, 0], jnp.transpose(forward_e[0, 0], (1, 0, 2)), n_x, n_y,
    )
    products = products.reshape(STEPS, sources, capacity)
    segments = recv_param.reshape(sources, capacity)
    if sources & (sources - 1) == 0:
        received, segments = exchange_by_halving(products, segments, sources)
    else:
        received = lax.all_to_all(products, "slab", split_axis=1, concat_axis=1, tiled=True)
    segments = jnp.broadcast_to(segments[None], received.shape).reshape(-1, 1)
    params = lax.broadcasted_iota(jnp.int32, (1, PAR_DEV), 1)
    gradient = jnp.sum(jnp.where(segments == params, received.reshape(-1, 1), 0.0), axis=0)
    return (new_e, new_h, gradient.reshape(1, 1, PAR_DEV))


def solution(mesh):
    return jax.shard_map(
        shards,
        mesh=mesh,
        in_specs=(
            P(None, "slab", "yz", None),
            P(None, "slab", "yz", None),
            P(None, "slab", "yz", None),
            P("slab", "yz", None),
            P("slab", "yz", None, None, None),
            P("slab", "yz", None, None),
            P("slab", "yz", None, None),
        ),
        out_specs=(P(None, "slab", "yz", None), P(None, "slab", "yz", None), P("slab", "yz", None)),
        check_vma=False,
    )
```

```python
import functools

import jax
import jax.numpy as jnp
from jax import lax
from jax.experimental import pallas as pl
from jax.experimental.pallas import tpu as pltpu
from jax.sharding import PartitionSpec as P

STEPS = 2
PAR_DEV = 128
HALO = 2
LANES = 128
RADIX = 4

CH_GAIN = 0.5
CE_GAIN = 0.5


def recv_from(array, axis, offset):
    count = lax.axis_size(axis)
    pairs = [(i + offset, i) for i in range(count) if 0 <= i + offset < count]
    return lax.ppermute(array, axis, pairs)


def ahead(values, axis):
    extent = values.shape[axis]
    if axis == 0:
        return jnp.concatenate([values[1:], values[:1]], 0)
    shifted = pltpu.roll(values, extent - 1, axis)
    if axis == 2:
        lane = lax.broadcasted_iota(jnp.int32, values.shape, 2)
        shifted = jnp.where(lane == extent - 1, 0.0, shifted)
    return shifted


def behind(values, axis):
    extent = values.shape[axis]
    if axis == 0:
        return jnp.concatenate([values[extent - 1 :], values[: extent - 1]], 0)
    shifted = pltpu.roll(values, 1, axis)
    if axis == 2:
        lane = lax.broadcasted_iota(jnp.int32, values.shape, 2)
        shifted = jnp.where(lane == 0, 0.0, shifted)
    return shifted


def swap_halos(first, last, axis):
    count = lax.axis_size(axis)
    odd = lax.axis_index(axis) % 2 == 1
    inner = [(i, i ^ 1) for i in range(count) if i ^ 1 < count]
    outer = [p for i in range(1, count - 1, 2) for p in ((i, i + 1), (i + 1, i))]
    got_inner = lax.ppermute(jnp.where(odd, first, last), axis, inner)
    got_outer = lax.ppermute(jnp.where(odd, last, first), axis, outer)
    return got_inner, got_outer


def low_high(got_inner, got_outer, odd):
    return jnp.where(odd, got_inner, got_outer), jnp.where(odd, got_outer, got_inner)


def leapfrog_kernel(
    dims, e_ref, h_ref, perm_ref, cond_ref, x_inner_ref, x_outer_ref, y_inner_ref, y_outer_ref,
    cell_ref, fwd_ref, e_out, h_out, prod_out, ring,
):
    depth_x, depth_y, n_x, n_y = dims
    ring_x, ring_y = ring.shape[1], ring.shape[2]
    slab, yz = lax.axis_index("slab"), lax.axis_index("yz")
    xlo, xhi = low_high(x_inner_ref[...], x_outer_ref[...], slab % 2 == 1)
    ylo, yhi = low_high(y_inner_ref[...], y_outer_ref[...], yz % 2 == 1)
    y_far = {depth_y: depth_y + 1, ring_y - 1: ring_y - 2}
    ring[0:3, 0:depth_x, 0:depth_y] = e_ref[...]
    ring[3:6, 0:depth_x, 0:depth_y] = h_ref[...]
    ring[6:9, 0:depth_x, 0:depth_y] = perm_ref[...]
    ring[9:10, 0:depth_x, 0:depth_y] = cond_ref[...]
    ring[:, depth_x : depth_x + HALO, 0:depth_y] = xhi
    ring[:, ring_x - HALO : ring_x, 0:depth_y] = xlo
    ring[:, :, depth_y:ring_y] = jnp.zeros((ring.shape[0], ring_x, ring_y - depth_y, LANES), jnp.float32)
    for piece, first, near in ((yhi, depth_y, depth_y), (ylo, ring_y - HALO, ring_y - 1)):
        for c in range(6):
            for r in range(HALO):
                for x in range(ring_x):
                    ring[c, x, first + r : first + r + 1, :] = piece[2 * c + r, x : x + 1, :]
        for c in range(4):
            for x in range(ring_x):
                ring[6 + c, x, near : near + 1, :] = piece[12 + c, x : x + 1, :]
        for x in range(ring_x):
            ring[6:9, x, y_far[near] : y_far[near] + 1, :] = jnp.ones((3, 1, LANES), jnp.float32)

    shape = (ring_x, ring_y, LANES)
    xi = lax.broadcasted_iota(jnp.int32, shape, 0)
    yi = lax.broadcasted_iota(jnp.int32, shape, 1)
    gx = slab * depth_x + jnp.where(xi < depth_x + HALO, xi, xi - ring_x)
    gy = yz * depth_y + jnp.where(yi < depth_y + HALO, yi, yi - ring_y)
    y_real = (yi < depth_y + HALO) | (yi >= ring_y - HALO)
    inside = (gx >= 0) & (gx < n_x) & (gy >= 0) & (gy < n_y) & y_real

    field_e = [ring[c] for c in range(3)]
    field_h = [ring[3 + c] for c in range(3)]
    conductivity = ring[9]
    keep_rate, curl_gain = [], []
    for c in range(3):
        permittivity = jnp.where(inside, ring[6 + c], 1.0)
        ratio = 0.5 * conductivity / permittivity
        keep_rate.append((1.0 - ratio) / (1.0 + ratio))
        curl_gain.append(CE_GAIN / (permittivity * (1.0 + ratio)))

    grid = cell_ref[...].astype(jnp.float32)
    owners, capacity = grid.shape
    slots = owners * capacity
    slot = lax.broadcasted_iota(jnp.int32, (capacity, slots), 1)
    spread = (slot % capacity == lax.broadcasted_iota(jnp.int32, (capacity, slots), 0)).astype(jnp.float32)
    by_owner = jnp.dot(grid, spread, precision=lax.Precision.HIGHEST, preferred_element_type=jnp.float32)
    mine = lax.broadcasted_iota(jnp.int32, (owners, slots), 1) // capacity == lax.broadcasted_iota(
        jnp.int32, (owners, slots), 0
    )
    cells = jnp.sum(jnp.where(mine, by_owner, 0.0), axis=0, keepdims=True).astype(jnp.int32)
    rows = depth_x * depth_y
    lane_pick = (lax.broadcasted_iota(jnp.int32, (LANES, cells.shape[1]), 0) == (cells % LANES)).astype(jnp.float32)
    row_pick = lax.broadcasted_iota(jnp.int32, (rows, cells.shape[1]), 0) == (cells // LANES)

    for step_index in range(STEPS):
        e0, e1, e2 = field_e
        curl = (
            (ahead(e2, 1) - e2) - (ahead(e1, 2) - e1),
            (ahead(e0, 2) - e0) - (ahead(e2, 0) - e2),
            (ahead(e1, 0) - e1) - (ahead(e0, 1) - e0),
        )
        field_h = [jnp.where(inside, field_h[c] - CH_GAIN * curl[c], 0.0) for c in range(3)]
        h0, h1, h2 = field_h
        curl = (
            (h2 - behind(h2, 1)) - (h1 - behind(h1, 2)),
            (h0 - behind(h0, 2)) - (h2 - behind(h2, 0)),
            (h1 - behind(h1, 0)) - (h0 - behind(h0, 1)),
        )
        field_e = [
            jnp.where(inside, keep_rate[c] * field_e[c] + curl_gain[c] * curl[c], 0.0) for c in range(3)
        ]
        product = None
        for c in range(3):
            block = field_e[c][0:depth_x, 0:depth_y].reshape(rows, LANES)
            by_lane = jnp.dot(block, lane_pick, precision=lax.Precision.HIGHEST, preferred_element_type=jnp.float32)
            picked = jnp.sum(jnp.where(row_pick, by_lane, 0.0), axis=0, keepdims=True)
            term = picked * fwd_ref[c, step_index : step_index + 1, :]
            product = term if product is None else product + term
        prod_out[step_index : step_index + 1, :] = product

    for c in range(3):
        e_out[c] = field_e[c][0:depth_x, 0:depth_y]
        h_out[c] = field_h[c][0:depth_x, 0:depth_y]


def leapfrog(field_e, field_h, permittivity, conductivity, xlo, xhi, ylo, yhi, cells, fwd, n_x, n_y):
    _, depth_x, depth_y, _ = field_e.shape
    ring_x = depth_x + 2 * HALO
    ring_y = -(-(depth_y + 2 * HALO) // 8) * 8
    vmem = pl.BlockSpec(memory_space=pltpu.VMEM)
    kernel = functools.partial(leapfrog_kernel, (depth_x, depth_y, n_x, n_y))
    return pl.pallas_call(
        kernel,
        out_shape=(
            jax.ShapeDtypeStruct(field_e.shape, jnp.float32),
            jax.ShapeDtypeStruct(field_h.shape, jnp.float32),
            jax.ShapeDtypeStruct((STEPS, cells.size), jnp.float32),
        ),
        in_specs=[vmem] * 10,
        out_specs=(vmem, vmem, vmem),
        scratch_shapes=[pltpu.VMEM((10, ring_x, ring_y, LANES), jnp.float32)],
    )(field_e, field_h, permittivity, conductivity, xlo, xhi, ylo, yhi, cells, fwd)


def xor_rows(array, me, count, axis):
    bit = 1
    while bit < count:
        shape = array.shape[:axis] + (count // (2 * bit), 2, bit) + array.shape[axis + 1 :]
        split = array.reshape(shape)
        swapped = jnp.flip(split, axis + 1).reshape(array.shape)
        array = jnp.where((me // bit) % 2 == 1, swapped, array)
        bit *= 2
    return array


def exchange_by_halving(products, segments, count):
    me = lax.axis_index("slab")
    held = xor_rows(products, me, count, 1)[:, :, None]
    bit = count // 2
    while bit >= RADIX:
        owners = held.shape[1]
        keep = held[:, : owners // 2]
        send = held[:, owners // 2 :]
        pairs = [(i, i ^ bit) for i in range(count)]
        got = lax.ppermute(send, "slab", pairs)
        held = jnp.stack([keep, got], 3).reshape(keep.shape[:2] + (keep.shape[2] * 2,) + keep.shape[3:])
        bit //= 2
    owners = held.shape[1]
    pieces = [held[:, 0]]
    for q in range(1, owners):
        pieces.append(lax.ppermute(held[:, q], "slab", [(i, i ^ q) for i in range(count)]))
    held = jnp.stack(pieces, 2)
    held = held.reshape(held.shape[:1] + (held.shape[1] * owners,) + held.shape[3:])
    return held, xor_rows(segments, me, count, 0)


def shards(field_e, field_h, permittivity, conductivity, forward_e, slot_cell, recv_param):
    depth_x = field_e.shape[1]
    depth_y = field_e.shape[2]
    sources = recv_param.shape[2]
    capacity = recv_param.shape[3]
    n_x = lax.axis_size("slab") * depth_x
    n_y = lax.axis_size("yz") * depth_y
    parts = (field_e, field_h, permittivity, conductivity[None])
    x_inner, x_outer = swap_halos(
        jnp.concatenate([p[:, :HALO] for p in parts], 0),
        jnp.concatenate([p[:, depth_x - HALO :] for p in parts], 0),
        "slab",
    )
    xlo, xhi = low_high(x_inner, x_outer, lax.axis_index("slab") % 2 == 1)
    def rows(start, near):
        stack = jnp.concatenate(parts, 0)
        stack = jnp.concatenate([stack, xhi, xlo], 1)
        fields = [stack[c, :, start + r] for c in range(6) for r in range(HALO)]
        material = [stack[c, :, start + near] for c in range(6, 10)]
        return jnp.stack(fields + material)

    y_inner, y_outer = swap_halos(rows(0, 0), rows(depth_y - HALO, HALO - 1), "yz")
    new_e, new_h, products = leapfrog(
        field_e, field_h, permittivity, conductivity[None], x_inner, x_outer, y_inner, y_outer,
        slot_cell[0, 0], jnp.transpose(forward_e[0, 0], (1, 0, 2)), n_x, n_y,
    )
    products = products.reshape(STEPS, sources, capacity)
    segments = recv_param.reshape(sources, capacity)
    if sources & (sources - 1) == 0:
        received, segments = exchange_by_halving(products, segments, sources)
    else:
        received = lax.all_to_all(products, "slab", split_axis=1, concat_axis=1, tiled=True)
    segments = jnp.broadcast_to(segments[None], received.shape).reshape(-1, 1)
    params = lax.broadcasted_iota(jnp.int32, (1, PAR_DEV), 1)
    gradient = jnp.sum(jnp.where(segments == params, received.reshape(-1, 1), 0.0), axis=0)
    return (new_e, new_h, gradient.reshape(1, 1, PAR_DEV))


def solution(mesh):
    return jax.shard_map(
        shards,
        mesh=mesh,
        in_specs=(
            P(None, "slab", "yz", None),
            P(None, "slab", "yz", None),
            P(None, "slab", "yz", None),
            P("slab", "yz", None),
            P("slab", "yz", None, None, None),
            P("slab", "yz", None, None),
            P("slab", "yz", None, None),
        ),
        out_specs=(P(None, "slab", "yz", None), P(None, "slab", "yz", None), P("slab", "yz", None)),
        check_vma=False,
    )
```

```python
import functools

import jax
import jax.numpy as jnp
from jax import lax
from jax.experimental import pallas as pl
from jax.experimental.pallas import tpu as pltpu
from jax.sharding import PartitionSpec as P

STEPS = 2
PAR_DEV = 128
HALO = 2
LANES = 128
RADIX = 4

CH_GAIN = 0.5
CE_GAIN = 0.5


def recv_from(array, axis, offset):
    count = lax.axis_size(axis)
    pairs = [(i + offset, i) for i in range(count) if 0 <= i + offset < count]
    return lax.ppermute(array, axis, pairs)


def ahead(values, axis):
    extent = values.shape[axis]
    if axis == 0:
        return jnp.concatenate([values[1:], values[:1]], 0)
    shifted = pltpu.roll(values, extent - 1, axis)
    if axis == 2:
        lane = lax.broadcasted_iota(jnp.int32, values.shape, 2)
        shifted = jnp.where(lane == extent - 1, 0.0, shifted)
    return shifted


def behind(values, axis):
    extent = values.shape[axis]
    if axis == 0:
        return jnp.concatenate([values[extent - 1 :], values[: extent - 1]], 0)
    shifted = pltpu.roll(values, 1, axis)
    if axis == 2:
        lane = lax.broadcasted_iota(jnp.int32, values.shape, 2)
        shifted = jnp.where(lane == 0, 0.0, shifted)
    return shifted


def swap_halos(first, last, axis):
    count = lax.axis_size(axis)
    odd = lax.axis_index(axis) % 2 == 1
    inner = [(i, i ^ 1) for i in range(count) if i ^ 1 < count]
    outer = [p for i in range(1, count - 1, 2) for p in ((i, i + 1), (i + 1, i))]
    got_inner = lax.ppermute(jnp.where(odd, first, last), axis, inner)
    got_outer = lax.ppermute(jnp.where(odd, last, first), axis, outer)
    return got_inner, got_outer


def low_high(got_inner, got_outer, odd):
    return jnp.where(odd, got_inner, got_outer), jnp.where(odd, got_outer, got_inner)


def leapfrog_kernel(
    dims, e_ref, h_ref, perm_ref, cond_ref, x_inner_ref, x_outer_ref, y_inner_ref, y_outer_ref,
    y_inner2_ref, y_outer2_ref, cell_ref, fwd_ref, e_out, h_out, prod_out, ring,
):
    depth_x, depth_y, n_x, n_y = dims
    ring_x, ring_y = ring.shape[1], ring.shape[2]
    slab, yz = lax.axis_index("slab"), lax.axis_index("yz")
    xlo, xhi = low_high(x_inner_ref[...], x_outer_ref[...], slab % 2 == 1)
    y_inner = jnp.concatenate([y_inner_ref[...], y_inner2_ref[...]], 0)
    y_outer = jnp.concatenate([y_outer_ref[...], y_outer2_ref[...]], 0)
    ylo, yhi = low_high(y_inner, y_outer, yz % 2 == 1)
    ring[0:3, 0:depth_x, 0:depth_y] = e_ref[...]
    ring[3:6, 0:depth_x, 0:depth_y] = h_ref[...]
    ring[6:9, 0:depth_x, 0:depth_y] = perm_ref[...]
    ring[9:10, 0:depth_x, 0:depth_y] = cond_ref[...]
    ring[:, depth_x : depth_x + HALO, 0:depth_y] = xhi
    ring[:, ring_x - HALO : ring_x, 0:depth_y] = xlo
    ring[:, :, depth_y : depth_y + HALO] = yhi
    ring[:, :, depth_y + HALO : ring_y - HALO] = jnp.zeros(
        (ring.shape[0], ring_x, ring_y - depth_y - 2 * HALO, LANES), jnp.float32
    )
    ring[:, :, ring_y - HALO : ring_y] = ylo

    shape = (ring_x, ring_y, LANES)
    xi = lax.broadcasted_iota(jnp.int32, shape, 0)
    yi = lax.broadcasted_iota(jnp.int32, shape, 1)
    gx = slab * depth_x + jnp.where(xi < depth_x + HALO, xi, xi - ring_x)
    gy = yz * depth_y + jnp.where(yi < depth_y + HALO, yi, yi - ring_y)
    y_real = (yi < depth_y + HALO) | (yi >= ring_y - HALO)
    inside = (gx >= 0) & (gx < n_x) & (gy >= 0) & (gy < n_y) & y_real

    field_e = [ring[c] for c in range(3)]
    field_h = [ring[3 + c] for c in range(3)]
    conductivity = ring[9]
    keep_rate, curl_gain = [], []
    for c in range(3):
        permittivity = jnp.where(inside, ring[6 + c], 1.0)
        ratio = 0.5 * conductivity / permittivity
        keep_rate.append((1.0 - ratio) / (1.0 + ratio))
        curl_gain.append(CE_GAIN / (permittivity * (1.0 + ratio)))

    grid = cell_ref[...].astype(jnp.float32)
    owners, capacity = grid.shape
    slots = owners * capacity
    slot = lax.broadcasted_iota(jnp.int32, (capacity, slots), 1)
    spread = (slot % capacity == lax.broadcasted_iota(jnp.int32, (capacity, slots), 0)).astype(jnp.float32)
    by_owner = jnp.dot(grid, spread, precision=lax.Precision.HIGHEST, preferred_element_type=jnp.float32)
    mine = lax.broadcasted_iota(jnp.int32, (owners, slots), 1) // capacity == lax.broadcasted_iota(
        jnp.int32, (owners, slots), 0
    )
    cells = jnp.sum(jnp.where(mine, by_owner, 0.0), axis=0, keepdims=True).astype(jnp.int32)
    rows = depth_x * depth_y
    lane_pick = (lax.broadcasted_iota(jnp.int32, (LANES, cells.shape[1]), 0) == (cells % LANES)).astype(jnp.float32)
    row_pick = lax.broadcasted_iota(jnp.int32, (rows, cells.shape[1]), 0) == (cells // LANES)

    for step_index in range(STEPS):
        e0, e1, e2 = field_e
        curl = (
            (ahead(e2, 1) - e2) - (ahead(e1, 2) - e1),
            (ahead(e0, 2) - e0) - (ahead(e2, 0) - e2),
            (ahead(e1, 0) - e1) - (ahead(e0, 1) - e0),
        )
        field_h = [jnp.where(inside, field_h[c] - CH_GAIN * curl[c], 0.0) for c in range(3)]
        h0, h1, h2 = field_h
        curl = (
            (h2 - behind(h2, 1)) - (h1 - behind(h1, 2)),
            (h0 - behind(h0, 2)) - (h2 - behind(h2, 0)),
            (h1 - behind(h1, 0)) - (h0 - behind(h0, 1)),
        )
        field_e = [
            jnp.where(inside, keep_rate[c] * field_e[c] + curl_gain[c] * curl[c], 0.0) for c in range(3)
        ]
        product = None
        for c in range(3):
            block = field_e[c][0:depth_x, 0:depth_y].reshape(rows, LANES)
            by_lane = jnp.dot(block, lane_pick, precision=lax.Precision.HIGHEST, preferred_element_type=jnp.float32)
            picked = jnp.sum(jnp.where(row_pick, by_lane, 0.0), axis=0, keepdims=True)
            term = picked * fwd_ref[c, step_index : step_index + 1, :]
            product = term if product is None else product + term
        prod_out[step_index : step_index + 1, :] = product

    for c in range(3):
        e_out[c] = field_e[c][0:depth_x, 0:depth_y]
        h_out[c] = field_h[c][0:depth_x, 0:depth_y]


def leapfrog(field_e, field_h, permittivity, conductivity, xlo, xhi, ylo, yhi, ylo2, yhi2, cells, fwd, n_x, n_y):
    _, depth_x, depth_y, _ = field_e.shape
    ring_x = depth_x + 2 * HALO
    ring_y = -(-(depth_y + 2 * HALO) // 8) * 8
    vmem = pl.BlockSpec(memory_space=pltpu.VMEM)
    kernel = functools.partial(leapfrog_kernel, (depth_x, depth_y, n_x, n_y))
    return pl.pallas_call(
        kernel,
        out_shape=(
            jax.ShapeDtypeStruct(field_e.shape, jnp.float32),
            jax.ShapeDtypeStruct(field_h.shape, jnp.float32),
            jax.ShapeDtypeStruct((STEPS, cells.size), jnp.float32),
        ),
        in_specs=[vmem] * 12,
        out_specs=(vmem, vmem, vmem),
        scratch_shapes=[pltpu.VMEM((10, ring_x, ring_y, LANES), jnp.float32)],
    )(field_e, field_h, permittivity, conductivity, xlo, xhi, ylo, yhi, ylo2, yhi2, cells, fwd)


def xor_rows(array, me, count, axis):
    bit = 1
    while bit < count:
        shape = array.shape[:axis] + (count // (2 * bit), 2, bit) + array.shape[axis + 1 :]
        split = array.reshape(shape)
        swapped = jnp.flip(split, axis + 1).reshape(array.shape)
        array = jnp.where((me // bit) % 2 == 1, swapped, array)
        bit *= 2
    return array


def exchange_by_halving(products, segments, count):
    me = lax.axis_index("slab")
    held = xor_rows(products, me, count, 1)[:, :, None]
    bit = count // 2
    while bit >= RADIX:
        owners = held.shape[1]
        keep = held[:, : owners // 2]
        send = held[:, owners // 2 :]
        pairs = [(i, i ^ bit) for i in range(count)]
        got = lax.ppermute(send, "slab", pairs)
        held = jnp.stack([keep, got], 3).reshape(keep.shape[:2] + (keep.shape[2] * 2,) + keep.shape[3:])
        bit //= 2
    owners = held.shape[1]
    pieces = [held[:, 0]]
    for q in range(1, owners):
        pieces.append(lax.ppermute(held[:, q], "slab", [(i, i ^ q) for i in range(count)]))
    held = jnp.stack(pieces, 2)
    held = held.reshape(held.shape[:1] + (held.shape[1] * owners,) + held.shape[3:])
    return held, xor_rows(segments, me, count, 0)


def shards(field_e, field_h, permittivity, conductivity, forward_e, slot_cell, recv_param):
    depth_x = field_e.shape[1]
    depth_y = field_e.shape[2]
    sources = recv_param.shape[2]
    capacity = recv_param.shape[3]
    n_x = lax.axis_size("slab") * depth_x
    n_y = lax.axis_size("yz") * depth_y
    parts = (field_e, field_h, permittivity, conductivity[None])
    x_inner, x_outer = swap_halos(
        jnp.concatenate([p[:, :HALO] for p in parts], 0),
        jnp.concatenate([p[:, depth_x - HALO :] for p in parts], 0),
        "slab",
    )
    xlo, xhi = low_high(x_inner, x_outer, lax.axis_index("slab") % 2 == 1)
    def rows(start):
        center = jnp.concatenate([p[:, :, start : start + HALO] for p in parts], 0)
        return jnp.concatenate([center, xhi[:, :, start : start + HALO], xlo[:, :, start : start + HALO]], 1)

    first, last = rows(0), rows(depth_y - HALO)
    split = first.shape[0] // 2
    y_inner, y_outer = swap_halos(first[:split], last[:split], "yz")
    y_inner2, y_outer2 = swap_halos(first[split:], last[split:], "yz")
    new_e, new_h, products = leapfrog(
        field_e, field_h, permittivity, conductivity[None], x_inner, x_outer, y_inner, y_outer, y_inner2, y_outer2,
        slot_cell[0, 0], jnp.transpose(forward_e[0, 0], (1, 0, 2)), n_x, n_y,
    )
    products = products.reshape(STEPS, sources, capacity)
    segments = recv_param.reshape(sources, capacity)
    if sources & (sources - 1) == 0:
        received, segments = exchange_by_halving(products, segments, sources)
    else:
        received = lax.all_to_all(products, "slab", split_axis=1, concat_axis=1, tiled=True)
    segments = jnp.broadcast_to(segments[None], received.shape).reshape(-1, 1)
    params = lax.broadcasted_iota(jnp.int32, (1, PAR_DEV), 1)
    gradient = jnp.sum(jnp.where(segments == params, received.reshape(-1, 1), 0.0), axis=0)
    return (new_e, new_h, gradient.reshape(1, 1, PAR_DEV))


def solution(mesh):
    return jax.shard_map(
        shards,
        mesh=mesh,
        in_specs=(
            P(None, "slab", "yz", None),
            P(None, "slab", "yz", None),
            P(None, "slab", "yz", None),
            P("slab", "yz", None),
            P("slab", "yz", None, None, None),
            P("slab", "yz", None, None),
            P("slab", "yz", None, None),
        ),
        out_specs=(P(None, "slab", "yz", None), P(None, "slab", "yz", None), P("slab", "yz", None)),
        check_vma=False,
    )
```
